32 devices in a mesh: dp: 8 (over y, x, core), space: 4 (over z).
Axes of the slice: x: 2, y: 2, z: 4, core: 2. Of those that a mesh axis runs over, the one named last changes fastest.
Arguments:
- latents: bfloat16 [8, 33, 4, 8, 256], P('dp', None, 'space'), may hold values from -6 to 6
- lengths: int32 [8], P('dp'), may hold values from 9 to 33, as said below
- spatial_weight: bfloat16 [3, 3, 256, 256], replicated, may hold values from -0.125 to 0.125
- temporal_weight: bfloat16 [3, 256, 256], replicated, may hold values from -0.21875 to 0.21875
- critic_weight: bfloat16 [256, 256], replicated, may hold values from -0.375 to 0.375
- critic_head: float32 [256], replicated, may hold values from -5 to 5
- critic_frames: int32 [8, 8], P('dp'), may hold values from 0 to 32, as said below
- recon_grad: bfloat16 [8, 33, 8, 16, 256], P('dp', None, 'space'), may hold values from -6 to 6
Outputs:
- decoded: bfloat16 [8, 33, 8, 16, 256], P('dp', None, 'space')
- grad_spatial: float32 [589824], P(('dp', 'space'))
- grad_temporal: float32 [196608], P(('dp', 'space'))
The draws below stay inside these ranges and needn't reach their ends.
Inputs may be any that keep to these rules, and one draw needn't show every extreme that they name: `lengths`: some clip has exactly 33 live frames and some exactly 9. `critic_frames`: each entry names a live frame of its clip (below that clip's length); a frame may be named by several slots.
All inputs are finite; a program needn't handle non-finite values.
Results may differ from the reference program's by a relative error of at most 0.0055.
Values may be sent and summed in bfloat16 or wider, within the bound.
No kernel may reach another device: no remote copies, remote signals or barrier semaphores. Data moves between devices by JAX's collectives and lax.ppermute only.
A program may use at most 64 MiB of HBM per device.

```python
import math
import jax
import jax.numpy as jnp
from jax import lax

C = 256
DH = 256
FMAX = 33
MIN_LEN = 9
ROWS = 1
COLS = 8
CLIPS = 8
HU = 8
WU = 16
SLOTS = 8
N_SPACE = 4


def clip_table(key):
    folded = jax.random.fold_in(key, 11)
    subkeys = jax.random.split(folded, 4)
    counts = jax.random.randint(subkeys[0], (CLIPS,), MIN_LEN, FMAX + 1)
    longest = jax.random.randint(subkeys[1], (), 0, CLIPS)
    stride = jax.random.randint(subkeys[2], (), 1, CLIPS)
    shortest = (longest + stride) % CLIPS
    counts = counts.at[longest].set(FMAX).at[shortest].set(MIN_LEN)
    chosen = jax.random.randint(subkeys[3], (CLIPS, SLOTS), 0, counts[:, None])
    chosen = chosen.at[longest, 0].set(FMAX - 1).at[shortest, 1].set(0)
    return (counts.astype(jnp.int32), chosen.astype(jnp.int32))


def draw_lengths(key, part):
    return clip_table(key)[0]


def draw_critic_frames(key, part):
    return clip_table(key)[1]


def block_levels(key, extent, cuts, low, high):
    gain, own = 1.0, jax.random.fold_in(key, 6)
    for axis_at, blocks in cuts:
        steps = jnp.exp(jax.random.uniform(jax.random.fold_in(own, axis_at), (blocks,), jnp.float32, low / len(cuts), high / len(cuts)))
        gain = gain * jnp.repeat(steps, extent[axis_at] // blocks).reshape([-1 if axis == axis_at else 1 for axis in range(len(extent))])
    return gain


def scatter_about(rng, dims, deviation, bound, cuts=(), dtype=jnp.bfloat16):
    values = jax.random.normal(rng, dims, jnp.float32) * deviation
    if len(cuts) > 0:
        values = block_levels(rng, dims, cuts, -0.22, 0.18) * values
    return jnp.clip(values, min=-bound, max=bound).astype(dtype)


def setup_inputs(seed: int = 0) -> dict:
    keys = jax.random.split(jax.random.key(seed), 9)
    return {
        "latents": scatter_about(keys[0], (CLIPS, FMAX, ROWS * N_SPACE, COLS, C), 1.0, 6.0, ((0, 8), (2, 4))),
        "lengths": draw_lengths(jax.random.fold_in(keys[8], 71), 0),
        "spatial_weight": scatter_about(keys[2], (3, 3, C, C), (9 * C) ** -0.5, 0.125),
        "temporal_weight": scatter_about(keys[3], (3, C, C), (3 * C) ** -0.5, 0.21875),
        "critic_weight": scatter_about(keys[4], (C, DH), C ** -0.5, 0.375),
        "critic_head": scatter_about(keys[5], (DH,), 1.0, 5.0, (), jnp.float32),
        "critic_frames": draw_critic_frames(jax.random.fold_in(keys[8], 71), 0),
        "recon_grad": scatter_about(keys[7], (CLIPS, FMAX, HU, WU, C), 1.0, 6.0, ((0, 8), (2, 4))),
    }


def upsample(values):
    doubled = jnp.repeat(values, 2, axis=-3)
    return jnp.repeat(doubled, 2, axis=-2)

def silu_slope(pre_act):
    sigmoid_val = jax.nn.sigmoid(pre_act)
    return sigmoid_val * (1.0 + pre_act * (1.0 - sigmoid_val))

def delayed(values, offset):
    if offset == 0:
        return values
    widths = [(0, 0)] * values.ndim
    widths[0] = (offset, 0)
    return jnp.pad(values, widths)[:values.shape[0]]

def advanced(values, offset):
    if offset == 0:
        return values
    widths = [(0, 0)] * values.ndim
    widths[0] = (0, offset)
    return jnp.pad(values, widths)[offset:]

def critic_slope(hidden, feature, critic_weight, critic_head):
    score_val = lax.optimization_barrier(jnp.sum(feature * critic_head, axis=-1))
    factor = -jax.nn.sigmoid(-score_val)[..., None] * critic_head
    unused, pullback = jax.vjp(jax.nn.gelu, hidden)
    gelu_slope = pullback(jnp.broadcast_to(factor[..., None, None, :], hidden.shape))[0].astype(jnp.bfloat16)
    return jnp.einsum('qhwe,ce->qhwc', gelu_slope.astype(jnp.float32), critic_weight.astype(jnp.float32))

def one_clip(latent, length, frames, recon_clip, spatial_weight, temporal_weight, critic_weight, critic_head):
    upsampled = upsample(latent)
    padded = jnp.pad(upsampled, ((0, 0), (1, 1), (1, 1), (0, 0)))
    height = upsampled.shape[1]
    width = upsampled.shape[2]
    pre_act = jnp.zeros(upsampled.shape, jnp.float32)
    for row_tap in range(3):
        for col_tap in range(3):
            window = padded[:, row_tap:row_tap + height, col_tap:col_tap + width].astype(jnp.float32)
            pre_act = pre_act + jnp.einsum('fhwc,cd->fhwd', window, spatial_weight[row_tap, col_tap].astype(jnp.float32))
    activated = jax.nn.silu(pre_act).astype(jnp.bfloat16)
    mixing = jnp.zeros(upsampled.shape, jnp.float32)
    for offset in range(3):
        mixing = mixing + jnp.einsum('fhwc,cd->fhwd', delayed(activated, offset).astype(jnp.float32), temporal_weight[offset].astype(jnp.float32))
    alive_mask = (jnp.arange(FMAX) < length).astype(jnp.float32)[:, None, None, None]
    decoded = (alive_mask * (upsampled.astype(jnp.float32) + mixing)).astype(jnp.bfloat16)
    chosen = decoded[frames].astype(jnp.float32)
    hidden = jnp.einsum('qhwc,ce->qhwe', chosen, critic_weight.astype(jnp.float32))
    feature = lax.optimization_barrier(jnp.mean(jax.nn.gelu(hidden), axis=(1, 2)))
    adverse_slots = critic_slope(hidden, feature, critic_weight, critic_head)
    adverse = jnp.zeros(decoded.shape, jnp.float32).at[frames].add(adverse_slots)
    loss_scale = 1.0 / math.sqrt(CLIPS * FMAX * HU * WU)
    cotangent = (alive_mask * loss_scale * (recon_clip.astype(jnp.float32) + adverse)).astype(jnp.bfloat16)
    cot_wide = cotangent.astype(jnp.float32)
    temporal_taps = []
    act_grad = jnp.zeros(upsampled.shape, jnp.float32)
    for offset in range(3):
        temporal_taps.append(jnp.einsum('fhwc,fhwd->cd', delayed(activated, offset).astype(jnp.float32), cot_wide))
        act_grad = act_grad + jnp.einsum('fhwd,cd->fhwc', advanced(cot_wide, offset), temporal_weight[offset].astype(jnp.float32))
    pre_slope = (act_grad * silu_slope(pre_act)).astype(jnp.bfloat16).astype(jnp.float32)
    spatial_taps = []
    for row_tap in range(3):
        for col_tap in range(3):
            window = padded[:, row_tap:row_tap + height, col_tap:col_tap + width].astype(jnp.float32)
            spatial_taps.append(jnp.einsum('fhwc,fhwd->cd', window, pre_slope))
    return (decoded, jnp.stack(spatial_taps).reshape(-1), jnp.stack(temporal_taps).reshape(-1))

def reference(latents, lengths, spatial_weight, temporal_weight, critic_weight, critic_head, critic_frames, recon_grad):

    def scan_clip(running, clip_items):
        latent, length, frames, recon_clip = clip_items
        decoded, spatial_grad, temporal_grad = one_clip(latent, length, frames, recon_clip, spatial_weight, temporal_weight, critic_weight, critic_head)
        return ((running[0] + spatial_grad, running[1] + temporal_grad), decoded)
    initial = (jnp.zeros((9 * C * C,), jnp.float32), jnp.zeros((3 * C * C,), jnp.float32))
    totals, decoded = lax.scan(scan_clip, initial, (latents, lengths, critic_frames, recon_grad))
    return (decoded, totals[0], totals[1])
```

```python
import math

import jax
import jax.numpy as jnp
from jax import lax
from jax.sharding import PartitionSpec as P


def _log2(n):
    b = n.bit_length() - 1
    return b if (1 << b) == n else None


def exchange_rows(cells, axis, dim):
    count = lax.axis_size(axis)
    ends = count - 1
    head = lax.slice_in_dim(cells, 0, 1, axis=dim)
    tail = lax.slice_in_dim(cells, cells.shape[dim] - 1, cells.shape[dim], axis=dim)
    above = lax.ppermute(tail, axis, [(i, i + 1) for i in range(ends)])
    below = lax.ppermute(head, axis, [(i + 1, i) for i in range(ends)])
    return above, below


def upsample(values):
    doubled = jnp.repeat(values, 2, axis=-3)
    return jnp.repeat(doubled, 2, axis=-2)


def silu_slope(pre_act):
    sigmoid_val = jax.nn.sigmoid(pre_act)
    return sigmoid_val * (1.0 + pre_act * (1.0 - sigmoid_val))


def delayed(values, offset):
    if offset == 0:
        return values
    widths = [(0, 0)] * values.ndim
    widths[1] = (offset, 0)
    return jnp.pad(values, widths)[:, : values.shape[1]]


def advanced(values, offset):
    if offset == 0:
        return values
    widths = [(0, 0)] * values.ndim
    widths[1] = (0, offset)
    return jnp.pad(values, widths)[:, offset:]


def space_sum(values):
    count = lax.axis_size("space")
    bits = _log2(count)
    if bits is None:
        return lax.psum(values, "space")
    for bit in range(bits):
        step = 1 << bit
        values = values + lax.ppermute(values, "space", [(i, i ^ step) for i in range(count)])
    return values


def halving_scatter(blocks):
    nd, ns = lax.axis_size("dp"), lax.axis_size("space")
    bd, bs = _log2(nd), _log2(ns)
    if bd is None or bs is None:
        flat = lax.psum_scatter(blocks.reshape(-1), "dp", scatter_dimension=0, tiled=True)
        return lax.psum_scatter(flat, "space", scatter_dimension=0, tiled=True)
    width = blocks.shape[1]
    dims = {("dp", i): bd - 1 - i for i in range(bd)}
    dims.update({("space", i): bd + bs - 1 - i for i in range(bs)})
    order = [("dp", i) for i in range(bd)] + [("space", i) for i in range(bs)]
    cur = jnp.transpose(
        blocks.reshape([2] * (bd + bs) + [width]), [dims[st] for st in order] + [bd + bs]
    )
    for axis, bit in order:
        size = nd if axis == "dp" else ns
        mine = (lax.axis_index(axis) // (1 << bit)) % 2
        keep = lax.dynamic_index_in_dim(cur, mine, 0, keepdims=False)
        send = lax.dynamic_index_in_dim(cur, 1 - mine, 0, keepdims=False)
        cur = keep + lax.ppermute(send, axis, [(i, i ^ (1 << bit)) for i in range(size)])
    return cur


def on_device(
    latents,
    lengths,
    spatial_weight,
    temporal_weight,
    critic_weight,
    critic_head,
    critic_frames,
    recon_grad,
):
    groups = lax.axis_size("space")
    devices = lax.axis_size("dp") * groups
    clip_count = latents.shape[0] * lax.axis_size("dp")
    frame_count = latents.shape[1]
    upsampled = upsample(latents)
    above, below = exchange_rows(latents, "space", 2)
    extended = jnp.concatenate(
        [upsample(above)[:, :, 1:], upsampled, upsample(below)[:, :, :1]], axis=2
    )
    padded = jnp.pad(extended, ((0, 0), (0, 0), (0, 0), (1, 1), (0, 0)))
    height = upsampled.shape[2]
    width = upsampled.shape[3]
    pre_act = jnp.zeros(upsampled.shape, jnp.float32)
    for row_tap in range(3):
        for col_tap in range(3):
            window = padded[:, :, row_tap : row_tap + height, col_tap : col_tap + width]
            pre_act = pre_act + jnp.einsum(
                "nfhwc,cd->nfhwd",
                window,
                spatial_weight[row_tap, col_tap],
                preferred_element_type=jnp.float32,
            )
    activated = jax.nn.silu(pre_act).astype(jnp.bfloat16)
    mixing = jnp.zeros(upsampled.shape, jnp.float32)
    for offset in range(3):
        mixing = mixing + jnp.einsum(
            "nfhwc,cd->nfhwd",
            delayed(activated, offset),
            temporal_weight[offset],
            preferred_element_type=jnp.float32,
        )
    alive_mask = (jnp.arange(frame_count)[None, :] < lengths[:, None]).astype(jnp.float32)[
        :, :, None, None, None
    ]
    decoded = (alive_mask * (upsampled.astype(jnp.float32) + mixing)).astype(jnp.bfloat16)
    chosen = jax.vmap(lambda clip_frames, indices: jnp.take(clip_frames, indices, axis=0))(
        decoded, critic_frames
    )
    hidden = jnp.einsum(
        "nqhwc,ce->nqhwe", chosen, critic_weight, preferred_element_type=jnp.float32
    )
    feature = space_sum(jnp.sum(jax.nn.gelu(hidden), axis=(2, 3))) / (height * groups * width)
    score_val = jnp.sum(feature * critic_head, axis=-1)
    factor = -jax.nn.sigmoid(-score_val)[..., None] * critic_head
    unused, pullback = jax.vjp(jax.nn.gelu, hidden)
    gelu_slope = pullback(jnp.broadcast_to(factor[..., None, None, :], hidden.shape))[0].astype(
        jnp.bfloat16
    )
    slope_rows = jnp.einsum(
        "nqhwe,ce->nqhwc", gelu_slope, critic_weight, preferred_element_type=jnp.float32
    )
    selector = (critic_frames[:, :, None] == jnp.arange(frame_count)[None, None, :]).astype(
        jnp.float32
    )
    adverse_frames = jnp.einsum(
        "nqf,nqhwc->nfhwc", selector, slope_rows, precision=lax.Precision.HIGHEST
    )
    loss_scale = 1.0 / math.sqrt(clip_count * frame_count * height * groups * width)
    cotangent = (
        alive_mask * loss_scale * (recon_grad.astype(jnp.float32) + adverse_frames)
    ).astype(jnp.bfloat16)
    temporal_grad = jnp.stack(
        [
            jnp.einsum(
                "nfhwc,nfhwd->cd",
                delayed(activated, offset),
                cotangent,
                preferred_element_type=jnp.float32,
            )
            for offset in range(3)
        ]
    )
    act_grad = jnp.zeros(upsampled.shape, jnp.float32)
    for offset in range(3):
        act_grad = act_grad + jnp.einsum(
            "nfhwd,cd->nfhwc",
            advanced(cotangent, offset),
            temporal_weight[offset],
            preferred_element_type=jnp.float32,
        )
    pre_slope = (act_grad * silu_slope(pre_act)).astype(jnp.bfloat16)
    tap_grads = []
    for row_tap in range(3):
        for col_tap in range(3):
            window = padded[:, :, row_tap : row_tap + height, col_tap : col_tap + width]
            tap_grads.append(
                jnp.einsum("nfhwc,nfhwd->cd", window, pre_slope, preferred_element_type=jnp.float32)
            )
    spatial_grad = jnp.stack(tap_grads).reshape(devices, -1)
    temporal_grad = temporal_grad.reshape(devices, -1)
    share = halving_scatter(jnp.concatenate([spatial_grad, temporal_grad], axis=1))
    spatial_width = spatial_grad.shape[1]
    return (decoded, share[:spatial_width], share[spatial_width:])


def solution(mesh):
    placed = (
        P("dp", None, "space", None, None),
        P("dp"),
        P(),
        P(),
        P(),
        P(),
        P("dp", None),
        P("dp", None, "space", None, None),
    )
    return jax.shard_map(
        on_device,
        mesh=mesh,
        in_specs=placed,
        out_specs=(P("dp", None, "space", None, None), P(("dp", "space")), P(("dp", "space"))),
        check_vma=False,
    )
```

```python
import math

import jax
import jax.numpy as jnp
from jax import lax
from jax.sharding import PartitionSpec as P


def _log2(n):
    b = n.bit_length() - 1
    return b if (1 << b) == n else None


def exchange_rows(cells, axis, dim):
    count = lax.axis_size(axis)
    ends = count - 1
    head = lax.slice_in_dim(cells, 0, 1, axis=dim)
    tail = lax.slice_in_dim(cells, cells.shape[dim] - 1, cells.shape[dim], axis=dim)
    above = lax.ppermute(tail, axis, [(i, i + 1) for i in range(ends)])
    below = lax.ppermute(head, axis, [(i + 1, i) for i in range(ends)])
    return above, below


def upsample(values):
    doubled = jnp.repeat(values, 2, axis=-3)
    return jnp.repeat(doubled, 2, axis=-2)


def silu_slope(pre_act):
    sigmoid_val = jax.nn.sigmoid(pre_act)
    return sigmoid_val * (1.0 + pre_act * (1.0 - sigmoid_val))


def delayed(values, offset):
    if offset == 0:
        return values
    widths = [(0, 0)] * values.ndim
    widths[1] = (offset, 0)
    return jnp.pad(values, widths)[:, : values.shape[1]]


def advanced(values, offset):
    if offset == 0:
        return values
    widths = [(0, 0)] * values.ndim
    widths[1] = (0, offset)
    return jnp.pad(values, widths)[:, offset:]


def space_sum(values):
    count = lax.axis_size("space")
    bits = _log2(count)
    if bits is None:
        return lax.psum(values, "space")
    for bit in range(bits):
        step = 1 << bit
        values = values + lax.ppermute(values, "space", [(i, i ^ step) for i in range(count)])
    return values


def _halve(cur, left, axis, bit):
    size = lax.axis_size(axis)
    pos = left.index((axis, bit))
    hi, lo = 1 << pos, 1 << (len(left) - 1 - pos)
    mine = (lax.axis_index(axis) // (1 << bit)) % 2
    v = cur.reshape(hi, 2, lo * cur.shape[1])
    keep = lax.dynamic_index_in_dim(v, mine, 1, keepdims=False).reshape(hi * lo, -1)
    send = lax.dynamic_index_in_dim(v, 1 - mine, 1, keepdims=False).reshape(hi * lo, -1)
    left.remove((axis, bit))
    return keep + lax.ppermute(send, axis, [(i, i ^ (1 << bit)) for i in range(size)])


def halving_scatter(blocks, orders):
    nd, ns = lax.axis_size("dp"), lax.axis_size("space")
    bd, bs = _log2(nd), _log2(ns)
    if bd is None or bs is None:
        flat = lax.psum_scatter(blocks.reshape(-1), "dp", scatter_dimension=0, tiled=True)
        return lax.psum_scatter(flat, "space", scatter_dimension=0, tiled=True)
    natural = [("dp", i) for i in reversed(range(bd))] + [("space", i) for i in reversed(range(bs))]
    shared = 0
    while shared < len(natural) and all(o[shared] == orders[0][shared] for o in orders):
        shared += 1
    left = list(natural)
    cur = blocks
    for axis, bit in orders[0][:shared]:
        cur = _halve(cur, left, axis, bit)
    width = cur.shape[1] // len(orders)
    outs = []
    for p, order in enumerate(orders):
        part, part_left = cur[:, p * width : (p + 1) * width], list(left)
        for axis, bit in order[shared:]:
            part = _halve(part, part_left, axis, bit)
        outs.append(part.reshape(-1))
    return jnp.concatenate(outs)


def on_device(
    latents,
    lengths,
    spatial_weight,
    temporal_weight,
    critic_weight,
    critic_head,
    critic_frames,
    recon_grad,
):
    groups = lax.axis_size("space")
    devices = lax.axis_size("dp") * groups
    clip_count = latents.shape[0] * lax.axis_size("dp")
    frame_count = latents.shape[1]
    upsampled = upsample(latents)
    above, below = exchange_rows(latents, "space", 2)
    extended = jnp.concatenate(
        [upsample(above)[:, :, 1:], upsampled, upsample(below)[:, :, :1]], axis=2
    )
    padded = jnp.pad(extended, ((0, 0), (0, 0), (0, 0), (1, 1), (0, 0)))
    height = upsampled.shape[2]
    width = upsampled.shape[3]
    pre_act = jnp.zeros(upsampled.shape, jnp.float32)
    for row_tap in range(3):
        for col_tap in range(3):
            window = padded[:, :, row_tap : row_tap + height, col_tap : col_tap + width]
            pre_act = pre_act + jnp.einsum(
                "nfhwc,cd->nfhwd",
                window,
                spatial_weight[row_tap, col_tap],
                preferred_element_type=jnp.float32,
            )
    activated = jax.nn.silu(pre_act).astype(jnp.bfloat16)
    mixing = jnp.zeros(upsampled.shape, jnp.float32)
    for offset in range(3):
        mixing = mixing + jnp.einsum(
            "nfhwc,cd->nfhwd",
            delayed(activated, offset),
            temporal_weight[offset],
            preferred_element_type=jnp.float32,
        )
    alive_mask = (jnp.arange(frame_count)[None, :] < lengths[:, None]).astype(jnp.float32)[
        :, :, None, None, None
    ]
    decoded = (alive_mask * (upsampled.astype(jnp.float32) + mixing)).astype(jnp.bfloat16)
    chosen = jax.vmap(lambda clip_frames, indices: jnp.take(clip_frames, indices, axis=0))(
        decoded, critic_frames
    )
    hidden = jnp.einsum(
        "nqhwc,ce->nqhwe", chosen, critic_weight, preferred_element_type=jnp.float32
    )
    feature = space_sum(jnp.sum(jax.nn.gelu(hidden), axis=(2, 3))) / (height * groups * width)
    score_val = jnp.sum(feature * critic_head, axis=-1)
    factor = -jax.nn.sigmoid(-score_val)[..., None] * critic_head
    unused, pullback = jax.vjp(jax.nn.gelu, hidden)
    gelu_slope = pullback(jnp.broadcast_to(factor[..., None, None, :], hidden.shape))[0].astype(
        jnp.bfloat16
    )
    slope_rows = jnp.einsum(
        "nqhwe,ce->nqhwc", gelu_slope, critic_weight, preferred_element_type=jnp.float32
    )
    selector = (critic_frames[:, :, None] == jnp.arange(frame_count)[None, None, :]).astype(
        jnp.float32
    )
    adverse_frames = jnp.einsum(
        "nqf,nqhwc->nfhwc", selector, slope_rows, precision=lax.Precision.HIGHEST
    )
    loss_scale = 1.0 / math.sqrt(clip_count * frame_count * height * groups * width)
    cotangent = (
        alive_mask * loss_scale * (recon_grad.astype(jnp.float32) + adverse_frames)
    ).astype(jnp.bfloat16)
    delayed_all = jnp.concatenate([delayed(activated, offset) for offset in range(3)], axis=-1)
    temporal_grad = jnp.einsum(
        "nfhwc,nfhwd->cd", delayed_all, cotangent, preferred_element_type=jnp.float32
    )
    act_grad = jnp.zeros(upsampled.shape, jnp.float32)
    for offset in range(3):
        act_grad = act_grad + jnp.einsum(
            "nfhwd,cd->nfhwc",
            advanced(cotangent, offset),
            temporal_weight[offset],
            preferred_element_type=jnp.float32,
        )
    pre_slope = (act_grad * silu_slope(pre_act)).astype(jnp.bfloat16)
    windows = jnp.concatenate(
        [
            padded[:, :, row_tap : row_tap + height, col_tap : col_tap + width]
            for row_tap in range(3)
            for col_tap in range(3)
        ],
        axis=-1,
    )
    spatial_grad = jnp.einsum(
        "nfhwc,nfhwd->cd", windows, pre_slope, preferred_element_type=jnp.float32
    ).reshape(devices, -1)
    temporal_grad = temporal_grad.reshape(devices, -1)
    core, x_bit, y_bit = ("dp", 0), ("dp", 1), ("dp", 2)
    z_lo, z_hi = ("space", 0), ("space", 1)
    nd = lax.axis_size("dp")
    if nd == 8 and groups == 4:
        orders = ([core, x_bit, y_bit, z_lo, z_hi], [core, y_bit, x_bit, z_hi, z_lo])
    else:
        plain = [("dp", i) for i in range(nd.bit_length() - 1)]
        orders = (plain + [("space", i) for i in range(groups.bit_length() - 1)],)
    share = halving_scatter(jnp.concatenate([spatial_grad, temporal_grad], axis=1), orders)
    spatial_width = spatial_grad.shape[1]
    return (decoded, share[:spatial_width], share[spatial_width:])


def solution(mesh):
    placed = (
        P("dp", None, "space", None, None),
        P("dp"),
        P(),
        P(),
        P(),
        P(),
        P("dp", None),
        P("dp", None, "space", None, None),
    )
    return jax.shard_map(
        on_device,
        mesh=mesh,
        in_specs=placed,
        out_specs=(P("dp", None, "space", None, None), P(("dp", "space")), P(("dp", "space"))),
        check_vma=False,
    )
```

```python
import math

import jax
import jax.numpy as jnp
from jax import lax
from jax.sharding import PartitionSpec as P


def _log2(n):
    b = n.bit_length() - 1
    return b if (1 << b) == n else None


def exchange_rows(cells, axis, dim):
    count = lax.axis_size(axis)
    ends = count - 1
    head = lax.slice_in_dim(cells, 0, 1, axis=dim)
    tail = lax.slice_in_dim(cells, cells.shape[dim] - 1, cells.shape[dim], axis=dim)
    above = lax.ppermute(tail, axis, [(i, i + 1) for i in range(ends)])
    below = lax.ppermute(head, axis, [(i + 1, i) for i in range(ends)])
    return above, below


def upsample(values):
    doubled = jnp.repeat(values, 2, axis=-3)
    return jnp.repeat(doubled, 2, axis=-2)


def silu_slope(pre_act):
    sigmoid_val = jax.nn.sigmoid(pre_act)
    return sigmoid_val * (1.0 + pre_act * (1.0 - sigmoid_val))


def delayed(values, offset):
    if offset == 0:
        return values
    widths = [(0, 0)] * values.ndim
    widths[1] = (offset, 0)
    return jnp.pad(values, widths)[:, : values.shape[1]]


def advanced(values, offset):
    if offset == 0:
        return values
    widths = [(0, 0)] * values.ndim
    widths[1] = (0, offset)
    return jnp.pad(values, widths)[:, offset:]


def space_sum(values):
    count = lax.axis_size("space")
    bits = _log2(count)
    if bits is None:
        return lax.psum(values, "space")
    for bit in range(bits):
        step = 1 << bit
        values = values + lax.ppermute(values, "space", [(i, i ^ step) for i in range(count)])
    return values


def _halve(cur, left, axis, bit):
    size = lax.axis_size(axis)
    pos = left.index((axis, bit))
    hi, lo = 1 << pos, 1 << (len(left) - 1 - pos)
    mine = (lax.axis_index(axis) // (1 << bit)) % 2
    v = cur.reshape(hi, 2, lo * cur.shape[1])
    low, high = v[:, 0].reshape(hi * lo, -1), v[:, 1].reshape(hi * lo, -1)
    upper = mine == 1
    keep = jnp.where(upper, high, low)
    send = jnp.where(upper, low, high)
    left.remove((axis, bit))
    return keep + lax.ppermute(send, axis, [(i, i ^ (1 << bit)) for i in range(size)])


def halving_scatter(blocks, orders):
    nd, ns = lax.axis_size("dp"), lax.axis_size("space")
    bd, bs = _log2(nd), _log2(ns)
    if bd is None or bs is None:
        flat = lax.psum_scatter(blocks.reshape(-1), "dp", scatter_dimension=0, tiled=True)
        return lax.psum_scatter(flat, "space", scatter_dimension=0, tiled=True)
    natural = [("dp", i) for i in reversed(range(bd))] + [("space", i) for i in reversed(range(bs))]
    shared = 0
    while shared < len(natural) and all(o[shared] == orders[0][shared] for o in orders):
        shared += 1
    left = list(natural)
    cur = blocks
    for axis, bit in orders[0][:shared]:
        cur = _halve(cur, left, axis, bit)
    width = cur.shape[1] // len(orders)
    outs = []
    for p, order in enumerate(orders):
        part, part_left = cur[:, p * width : (p + 1) * width], list(left)
        for axis, bit in order[shared:]:
            part = _halve(part, part_left, axis, bit)
        outs.append(part.reshape(-1))
    return jnp.concatenate(outs)


def on_device(
    latents,
    lengths,
    spatial_weight,
    temporal_weight,
    critic_weight,
    critic_head,
    critic_frames,
    recon_grad,
):
    groups = lax.axis_size("space")
    devices = lax.axis_size("dp") * groups
    clip_count = latents.shape[0] * lax.axis_size("dp")
    frame_count = latents.shape[1]
    upsampled = upsample(latents)
    above, below = exchange_rows(latents, "space", 2)
    extended = jnp.concatenate(
        [upsample(above)[:, :, 1:], upsampled, upsample(below)[:, :, :1]], axis=2
    )
    padded = jnp.pad(extended, ((0, 0), (0, 0), (0, 0), (1, 1), (0, 0)))
    height = upsampled.shape[2]
    width = upsampled.shape[3]
    pre_act = jnp.zeros(upsampled.shape, jnp.float32)
    for row_tap in range(3):
        for col_tap in range(3):
            window = padded[:, :, row_tap : row_tap + height, col_tap : col_tap + width]
            pre_act = pre_act + jnp.einsum(
                "nfhwc,cd->nfhwd",
                window,
                spatial_weight[row_tap, col_tap],
                preferred_element_type=jnp.float32,
            )
    activated = jax.nn.silu(pre_act).astype(jnp.bfloat16)
    mixing = jnp.zeros(upsampled.shape, jnp.float32)
    for offset in range(3):
        mixing = mixing + jnp.einsum(
            "nfhwc,cd->nfhwd",
            delayed(activated, offset),
            temporal_weight[offset],
            preferred_element_type=jnp.float32,
        )
    alive_mask = (jnp.arange(frame_count)[None, :] < lengths[:, None]).astype(jnp.float32)[
        :, :, None, None, None
    ]
    decoded = (alive_mask * (upsampled.astype(jnp.float32) + mixing)).astype(jnp.bfloat16)
    chosen = jax.vmap(lambda clip_frames, indices: jnp.take(clip_frames, indices, axis=0))(
        decoded, critic_frames
    )
    hidden = jnp.einsum(
        "nqhwc,ce->nqhwe", chosen, critic_weight, preferred_element_type=jnp.float32
    )
    feature = space_sum(jnp.sum(jax.nn.gelu(hidden), axis=(2, 3))) / (height * groups * width)
    score_val = jnp.sum(feature * critic_head, axis=-1)
    factor = -jax.nn.sigmoid(-score_val)[..., None] * critic_head
    unused, pullback = jax.vjp(jax.nn.gelu, hidden)
    gelu_slope = pullback(jnp.broadcast_to(factor[..., None, None, :], hidden.shape))[0].astype(
        jnp.bfloat16
    )
    slope_rows = jnp.einsum(
        "nqhwe,ce->nqhwc", gelu_slope, critic_weight, preferred_element_type=jnp.float32
    )
    selector = (critic_frames[:, :, None] == jnp.arange(frame_count)[None, None, :]).astype(
        jnp.float32
    )
    adverse_frames = jnp.einsum(
        "nqf,nqhwc->nfhwc", selector, slope_rows, precision=lax.Precision.HIGHEST
    )
    loss_scale = 1.0 / math.sqrt(clip_count * frame_count * height * groups * width)
    cotangent = (
        alive_mask * loss_scale * (recon_grad.astype(jnp.float32) + adverse_frames)
    ).astype(jnp.bfloat16)
    temporal_grad = jnp.stack(
        [
            jnp.einsum(
                "nfhwc,nfhwd->cd",
                delayed(activated, offset),
                cotangent,
                preferred_element_type=jnp.float32,
            )
            for offset in range(3)
        ]
    )
    act_grad = jnp.zeros(upsampled.shape, jnp.float32)
    for offset in range(3):
        act_grad = act_grad + jnp.einsum(
            "nfhwd,cd->nfhwc",
            advanced(cotangent, offset),
            temporal_weight[offset],
            preferred_element_type=jnp.float32,
        )
    pre_slope = (act_grad * silu_slope(pre_act)).astype(jnp.bfloat16)
    tap_grads = []
    for row_tap in range(3):
        for col_tap in range(3):
            window = padded[:, :, row_tap : row_tap + height, col_tap : col_tap + width]
            tap_grads.append(
                jnp.einsum("nfhwc,nfhwd->cd", window, pre_slope, preferred_element_type=jnp.float32)
            )
    spatial_grad = jnp.stack(tap_grads).reshape(devices, -1)
    temporal_grad = temporal_grad.reshape(devices, -1)
    core, x_bit, y_bit = ("dp", 0), ("dp", 1), ("dp", 2)
    z_lo, z_hi = ("space", 0), ("space", 1)
    nd = lax.axis_size("dp")
    if nd == 8 and groups == 4:
        orders = ([core, x_bit, y_bit, z_lo, z_hi], [core, y_bit, x_bit, z_hi, z_lo])
    else:
        plain = [("dp", i) for i in range(nd.bit_length() - 1)]
        orders = (plain + [("space", i) for i in range(groups.bit_length() - 1)],)
    share = halving_scatter(jnp.concatenate([spatial_grad, temporal_grad], axis=1), orders)
    spatial_width = spatial_grad.shape[1]
    return (decoded, share[:spatial_width], share[spatial_width:])


def solution(mesh):
    placed = (
        P("dp", None, "space", None, None),
        P("dp"),
        P(),
        P(),
        P(),
        P(),
        P("dp", None),
        P("dp", None, "space", None, None),
    )
    return jax.shard_map(
        on_device,
        mesh=mesh,
        in_specs=placed,
        out_specs=(P("dp", None, "space", None, None), P(("dp", "space")), P(("dp", "space"))),
        check_vma=False,
    )
```

```python
import math

import jax
import jax.numpy as jnp
from jax import lax
from jax.sharding import PartitionSpec as P


def _log2(n):
    b = n.bit_length() - 1
    return b if (1 << b) == n else None


def exchange_rows(cells, axis, dim):
    count = lax.axis_size(axis)
    ends = count - 1
    head = lax.slice_in_dim(cells, 0, 1, axis=dim)
    tail = lax.slice_in_dim(cells, cells.shape[dim] - 1, cells.shape[dim], axis=dim)
    above = lax.ppermute(tail, axis, [(i, i + 1) for i in range(ends)])
    below = lax.ppermute(head, axis, [(i + 1, i) for i in range(ends)])
    return above, below


def upsample(values):
    doubled = jnp.repeat(values, 2, axis=-3)
    return jnp.repeat(doubled, 2, axis=-2)


def silu_slope(pre_act):
    sigmoid_val = jax.nn.sigmoid(pre_act)
    return sigmoid_val * (1.0 + pre_act * (1.0 - sigmoid_val))


def delayed(values, offset):
    if offset == 0:
        return values
    widths = [(0, 0)] * values.ndim
    widths[1] = (offset, 0)
    return jnp.pad(values, widths)[:, : values.shape[1]]


def advanced(values, offset):
    if offset == 0:
        return values
    widths = [(0, 0)] * values.ndim
    widths[1] = (0, offset)
    return jnp.pad(values, widths)[:, offset:]


def space_sum(values):
    count = lax.axis_size("space")
    bits = _log2(count)
    if bits is None:
        return lax.psum(values, "space")
    for bit in range(bits):
        step = 1 << bit
        values = values + lax.ppermute(values, "space", [(i, i ^ step) for i in range(count)])
    return values


def _halve(cur, left, axis, bit):
    size = lax.axis_size(axis)
    pos = left.index((axis, bit))
    hi, lo = 1 << pos, 1 << (len(left) - 1 - pos)
    mine = (lax.axis_index(axis) // (1 << bit)) % 2
    v = cur.reshape((hi, 2, lo) + cur.shape[1:])
    low, high = v[:, 0].reshape((hi * lo,) + cur.shape[1:]), v[:, 1].reshape((hi * lo,) + cur.shape[1:])
    upper = mine == 1
    keep = jnp.where(upper, high, low)
    send = jnp.where(upper, low, high)
    left.remove((axis, bit))
    return keep + lax.ppermute(send, axis, [(i, i ^ (1 << bit)) for i in range(size)])


def halving_scatter(blocks, orders):
    nd, ns = lax.axis_size("dp"), lax.axis_size("space")
    bd, bs = _log2(nd), _log2(ns)
    if bd is None or bs is None:
        flat = lax.psum_scatter(blocks, "dp", scatter_dimension=0, tiled=True)
        return lax.psum_scatter(flat, "space", scatter_dimension=0, tiled=True)[0]
    natural = [("dp", i) for i in reversed(range(bd))] + [("space", i) for i in reversed(range(bs))]
    shared = 0
    while shared < len(natural) and all(o[shared] == orders[0][shared] for o in orders):
        shared += 1
    left = list(natural)
    cur = blocks
    for axis, bit in orders[0][:shared]:
        cur = _halve(cur, left, axis, bit)
    width = cur.shape[1] // len(orders)
    outs = []
    for p, order in enumerate(orders):
        part, part_left = cur[:, p * width : (p + 1) * width], list(left)
        for axis, bit in order[shared:]:
            part = _halve(part, part_left, axis, bit)
        outs.append(part[0])
    return jnp.concatenate(outs)


def on_device(
    latents,
    lengths,
    spatial_weight,
    temporal_weight,
    critic_weight,
    critic_head,
    critic_frames,
    recon_grad,
):
    groups = lax.axis_size("space")
    devices = lax.axis_size("dp") * groups
    clip_count = latents.shape[0] * lax.axis_size("dp")
    frame_count = latents.shape[1]
    upsampled = upsample(latents)
    above, below = exchange_rows(latents, "space", 2)
    extended = jnp.concatenate(
        [upsample(above)[:, :, 1:], upsampled, upsample(below)[:, :, :1]], axis=2
    )
    padded = jnp.pad(extended, ((0, 0), (0, 0), (0, 0), (1, 1), (0, 0)))
    height = upsampled.shape[2]
    width = upsampled.shape[3]
    pre_act = jnp.zeros(upsampled.shape, jnp.float32)
    for row_tap in range(3):
        for col_tap in range(3):
            window = padded[:, :, row_tap : row_tap + height, col_tap : col_tap + width]
            pre_act = pre_act + jnp.einsum(
                "nfhwc,cd->nfhwd",
                window,
                spatial_weight[row_tap, col_tap],
                preferred_element_type=jnp.float32,
            )
    activated = jax.nn.silu(pre_act).astype(jnp.bfloat16)
    mixing = jnp.zeros(upsampled.shape, jnp.float32)
    for offset in range(3):
        mixing = mixing + jnp.einsum(
            "nfhwc,cd->nfhwd",
            delayed(activated, offset),
            temporal_weight[offset],
            preferred_element_type=jnp.float32,
        )
    alive_mask = (jnp.arange(frame_count)[None, :] < lengths[:, None]).astype(jnp.float32)[
        :, :, None, None, None
    ]
    decoded = (alive_mask * (upsampled.astype(jnp.float32) + mixing)).astype(jnp.bfloat16)
    chosen = jax.vmap(lambda clip_frames, indices: jnp.take(clip_frames, indices, axis=0))(
        decoded, critic_frames
    )
    hidden = jnp.einsum(
        "nqhwc,ce->nqhwe", chosen, critic_weight, preferred_element_type=jnp.float32
    )
    feature = space_sum(jnp.sum(jax.nn.gelu(hidden), axis=(2, 3))) / (height * groups * width)
    score_val = jnp.sum(feature * critic_head, axis=-1)
    factor = -jax.nn.sigmoid(-score_val)[..., None] * critic_head
    unused, pullback = jax.vjp(jax.nn.gelu, hidden)
    gelu_slope = pullback(jnp.broadcast_to(factor[..., None, None, :], hidden.shape))[0].astype(
        jnp.bfloat16
    )
    slope_rows = jnp.einsum(
        "nqhwe,ce->nqhwc", gelu_slope, critic_weight, preferred_element_type=jnp.float32
    )
    selector = (critic_frames[:, :, None] == jnp.arange(frame_count)[None, None, :]).astype(
        jnp.float32
    )
    adverse_frames = jnp.einsum(
        "nqf,nqhwc->nfhwc", selector, slope_rows, precision=lax.Precision.HIGHEST
    )
    loss_scale = 1.0 / math.sqrt(clip_count * frame_count * height * groups * width)
    cotangent = (
        alive_mask * loss_scale * (recon_grad.astype(jnp.float32) + adverse_frames)
    ).astype(jnp.bfloat16)
    temporal_grad = jnp.stack(
        [
            jnp.einsum(
                "nfhwc,nfhwd->cd",
                delayed(activated, offset),
                cotangent,
                preferred_element_type=jnp.float32,
            )
            for offset in range(3)
        ]
    )
    act_grad = jnp.zeros(upsampled.shape, jnp.float32)
    for offset in range(3):
        act_grad = act_grad + jnp.einsum(
            "nfhwd,cd->nfhwc",
            advanced(cotangent, offset),
            temporal_weight[offset],
            preferred_element_type=jnp.float32,
        )
    pre_slope = (act_grad * silu_slope(pre_act)).astype(jnp.bfloat16)
    tap_grads = []
    for row_tap in range(3):
        for col_tap in range(3):
            window = padded[:, :, row_tap : row_tap + height, col_tap : col_tap + width]
            tap_grads.append(
                jnp.einsum("nfhwc,nfhwd->cd", window, pre_slope, preferred_element_type=jnp.float32)
            )
    channels = spatial_weight.shape[-1]
    spatial_grad = jnp.stack(tap_grads).reshape(devices, -1, channels)
    temporal_grad = temporal_grad.reshape(devices, -1, channels)
    core, x_bit, y_bit = ("dp", 0), ("dp", 1), ("dp", 2)
    z_lo, z_hi = ("space", 0), ("space", 1)
    nd = lax.axis_size("dp")
    if nd == 8 and groups == 4:
        orders = ([core, x_bit, y_bit, z_lo, z_hi], [core, y_bit, x_bit, z_hi, z_lo])
    else:
        plain = [("dp", i) for i in range(nd.bit_length() - 1)]
        orders = (plain + [("space", i) for i in range(groups.bit_length() - 1)],)
    share = halving_scatter(jnp.concatenate([spatial_grad, temporal_grad], axis=1), orders)
    spatial_rows = spatial_grad.shape[1]
    return (decoded, share[:spatial_rows].reshape(-1), share[spatial_rows:].reshape(-1))


def solution(mesh):
    placed = (
        P("dp", None, "space", None, None),
        P("dp"),
        P(),
        P(),
        P(),
        P(),
        P("dp", None),
        P("dp", None, "space", None, None),
    )
    return jax.shard_map(
        on_device,
        mesh=mesh,
        in_specs=placed,
        out_specs=(P("dp", None, "space", None, None), P(("dp", "space")), P(("dp", "space"))),
        check_vma=False,
    )
```

```python
import math

import jax
import jax.numpy as jnp
from jax import lax
from jax.sharding import PartitionSpec as P


def _log2(n):
    b = n.bit_length() - 1
    return b if (1 << b) == n else None


def exchange_rows(cells, axis, dim):
    count = lax.axis_size(axis)
    ends = count - 1
    head = lax.slice_in_dim(cells, 0, 1, axis=dim)
    tail = lax.slice_in_dim(cells, cells.shape[dim] - 1, cells.shape[dim], axis=dim)
    above = lax.ppermute(tail, axis, [(i, i + 1) for i in range(ends)])
    below = lax.ppermute(head, axis, [(i + 1, i) for i in range(ends)])
    return above, below


def upsample(values):
    doubled = jnp.repeat(values, 2, axis=-3)
    return jnp.repeat(doubled, 2, axis=-2)


def silu_slope(pre_act):
    sigmoid_val = jax.nn.sigmoid(pre_act)
    return sigmoid_val * (1.0 + pre_act * (1.0 - sigmoid_val))


def delayed(values, offset):
    if offset == 0:
        return values
    widths = [(0, 0)] * values.ndim
    widths[1] = (offset, 0)
    return jnp.pad(values, widths)[:, : values.shape[1]]


def advanced(values, offset):
    if offset == 0:
        return values
    widths = [(0, 0)] * values.ndim
    widths[1] = (0, offset)
    return jnp.pad(values, widths)[:, offset:]


def space_sum(values):
    count = lax.axis_size("space")
    bits = _log2(count)
    if bits is None:
        return lax.psum(values, "space")
    for bit in range(bits):
        step = 1 << bit
        values = values + lax.ppermute(values, "space", [(i, i ^ step) for i in range(count)])
    return values


def _halve(cur, left, axis, bit):
    size = lax.axis_size(axis)
    pos = left.index((axis, bit))
    hi, lo = 1 << pos, 1 << (len(left) - 1 - pos)
    mine = (lax.axis_index(axis) // (1 << bit)) % 2
    v = cur.reshape((hi, 2, lo) + cur.shape[1:])
    low, high = v[:, 0].reshape((hi * lo,) + cur.shape[1:]), v[:, 1].reshape((hi * lo,) + cur.shape[1:])
    upper = mine == 1
    keep = jnp.where(upper, high, low)
    send = jnp.where(upper, low, high)
    left.remove((axis, bit))
    return keep + lax.ppermute(send, axis, [(i, i ^ (1 << bit)) for i in range(size)])


def halving_scatter(blocks, orders):
    nd, ns = lax.axis_size("dp"), lax.axis_size("space")
    bd, bs = _log2(nd), _log2(ns)
    if bd is None or bs is None:
        flat = lax.psum_scatter(blocks, "dp", scatter_dimension=0, tiled=True)
        return lax.psum_scatter(flat, "space", scatter_dimension=0, tiled=True)[0]
    natural = [("dp", i) for i in reversed(range(bd))] + [("space", i) for i in reversed(range(bs))]
    shared = 0
    while shared < len(natural) and all(o[shared] == orders[0][shared] for o in orders):
        shared += 1
    left = list(natural)
    cur = blocks
    for axis, bit in orders[0][:shared]:
        cur = _halve(cur, left, axis, bit)
    tail = len(natural)
    while tail > shared and all(o[tail - 1] == orders[0][tail - 1] for o in orders):
        tail -= 1
    width = cur.shape[1] // len(orders)
    outs = []
    for p, order in enumerate(orders):
        part, part_left = cur[:, p * width : (p + 1) * width], list(left)
        for axis, bit in order[shared:tail]:
            part = _halve(part, part_left, axis, bit)
        outs.append(part)
    cur = jnp.concatenate(outs, axis=1)
    for axis, bit in orders[0][tail:]:
        cur = _halve(cur, part_left, axis, bit)
    return cur[0]


def on_device(
    latents,
    lengths,
    spatial_weight,
    temporal_weight,
    critic_weight,
    critic_head,
    critic_frames,
    recon_grad,
):
    groups = lax.axis_size("space")
    devices = lax.axis_size("dp") * groups
    clip_count = latents.shape[0] * lax.axis_size("dp")
    frame_count = latents.shape[1]
    upsampled = upsample(latents)
    above, below = exchange_rows(latents, "space", 2)
    extended = jnp.concatenate(
        [upsample(above)[:, :, 1:], upsampled, upsample(below)[:, :, :1]], axis=2
    )
    padded = jnp.pad(extended, ((0, 0), (0, 0), (0, 0), (1, 1), (0, 0)))
    height = upsampled.shape[2]
    width = upsampled.shape[3]
    pre_act = jnp.zeros(upsampled.shape, jnp.float32)
    for row_tap in range(3):
        for col_tap in range(3):
            window = padded[:, :, row_tap : row_tap + height, col_tap : col_tap + width]
            pre_act = pre_act + jnp.einsum(
                "nfhwc,cd->nfhwd",
                window,
                spatial_weight[row_tap, col_tap],
                preferred_element_type=jnp.float32,
            )
    activated = jax.nn.silu(pre_act).astype(jnp.bfloat16)
    mixing = jnp.zeros(upsampled.shape, jnp.float32)
    for offset in range(3):
        mixing = mixing + jnp.einsum(
            "nfhwc,cd->nfhwd",
            delayed(activated, offset),
            temporal_weight[offset],
            preferred_element_type=jnp.float32,
        )
    alive_mask = (jnp.arange(frame_count)[None, :] < lengths[:, None]).astype(jnp.float32)[
        :, :, None, None, None
    ]
    decoded = (alive_mask * (upsampled.astype(jnp.float32) + mixing)).astype(jnp.bfloat16)
    chosen = jax.vmap(lambda clip_frames, indices: jnp.take(clip_frames, indices, axis=0))(
        decoded, critic_frames
    )
    hidden = jnp.einsum(
        "nqhwc,ce->nqhwe", chosen, critic_weight, preferred_element_type=jnp.float32
    )
    feature = space_sum(jnp.sum(jax.nn.gelu(hidden), axis=(2, 3))) / (height * groups * width)
    score_val = jnp.sum(feature * critic_head, axis=-1)
    factor = -jax.nn.sigmoid(-score_val)[..., None] * critic_head
    unused, pullback = jax.vjp(jax.nn.gelu, hidden)
    gelu_slope = pullback(jnp.broadcast_to(factor[..., None, None, :], hidden.shape))[0].astype(
        jnp.bfloat16
    )
    slope_rows = jnp.einsum(
        "nqhwe,ce->nqhwc", gelu_slope, critic_weight, preferred_element_type=jnp.float32
    )
    selector = (critic_frames[:, :, None] == jnp.arange(frame_count)[None, None, :]).astype(
        jnp.float32
    )
    adverse_frames = jnp.einsum(
        "nqf,nqhwc->nfhwc", selector, slope_rows, precision=lax.Precision.HIGHEST
    )
    loss_scale = 1.0 / math.sqrt(clip_count * frame_count * height * groups * width)
    cotangent = (
        alive_mask * loss_scale * (recon_grad.astype(jnp.float32) + adverse_frames)
    ).astype(jnp.bfloat16)
    temporal_grad = jnp.stack(
        [
            jnp.einsum(
                "nfhwc,nfhwd->cd",
                delayed(activated, offset),
                cotangent,
                preferred_element_type=jnp.float32,
            )
            for offset in range(3)
        ]
    )
    act_grad = jnp.zeros(upsampled.shape, jnp.float32)
    for offset in range(3):
        act_grad = act_grad + jnp.einsum(
            "nfhwd,cd->nfhwc",
            advanced(cotangent, offset),
            temporal_weight[offset],
            preferred_element_type=jnp.float32,
        )
    pre_slope = (act_grad * silu_slope(pre_act)).astype(jnp.bfloat16)
    tap_grads = []
    for row_tap in range(3):
        for col_tap in range(3):
            window = padded[:, :, row_tap : row_tap + height, col_tap : col_tap + width]
            tap_grads.append(
                jnp.einsum("nfhwc,nfhwd->cd", window, pre_slope, preferred_element_type=jnp.float32)
            )
    channels = spatial_weight.shape[-1]
    spatial_grad = jnp.stack(tap_grads).reshape(devices, -1, channels)
    temporal_grad = temporal_grad.reshape(devices, -1, channels)
    core, x_bit, y_bit = ("dp", 0), ("dp", 1), ("dp", 2)
    z_lo, z_hi = ("space", 0), ("space", 1)
    nd = lax.axis_size("dp")
    if nd == 8 and groups == 4:
        orders = ([core, x_bit, y_bit, z_lo, z_hi], [core, y_bit, x_bit, z_lo, z_hi])
    else:
        plain = [("dp", i) for i in range(nd.bit_length() - 1)]
        orders = (plain + [("space", i) for i in range(groups.bit_length() - 1)],)
    share = halving_scatter(jnp.concatenate([spatial_grad, temporal_grad], axis=1), orders)
    spatial_rows = spatial_grad.shape[1]
    return (decoded, share[:spatial_rows].reshape(-1), share[spatial_rows:].reshape(-1))


def solution(mesh):
    placed = (
        P("dp", None, "space", None, None),
        P("dp"),
        P(),
        P(),
        P(),
        P(),
        P("dp", None),
        P("dp", None, "space", None, None),
    )
    return jax.shard_map(
        on_device,
        mesh=mesh,
        in_specs=placed,
        out_specs=(P("dp", None, "space", None, None), P(("dp", "space")), P(("dp", "space"))),
        check_vma=False,
    )
```

```python
import math

import jax
import jax.numpy as jnp
from jax import lax
from jax.sharding import PartitionSpec as P


def _log2(n):
    b = n.bit_length() - 1
    return b if (1 << b) == n else None


def exchange_rows(cells, axis, dim):
    count = lax.axis_size(axis)
    ends = count - 1
    head = lax.slice_in_dim(cells, 0, 1, axis=dim)
    tail = lax.slice_in_dim(cells, cells.shape[dim] - 1, cells.shape[dim], axis=dim)
    above = lax.ppermute(tail, axis, [(i, i + 1) for i in range(ends)])
    below = lax.ppermute(head, axis, [(i + 1, i) for i in range(ends)])
    return above, below


def upsample(values):
    doubled = jnp.repeat(values, 2, axis=-3)
    return jnp.repeat(doubled, 2, axis=-2)


def silu_slope(pre_act):
    sigmoid_val = jax.nn.sigmoid(pre_act)
    return sigmoid_val * (1.0 + pre_act * (1.0 - sigmoid_val))


def delayed(values, offset):
    if offset == 0:
        return values
    widths = [(0, 0)] * values.ndim
    widths[1] = (offset, 0)
    return jnp.pad(values, widths)[:, : values.shape[1]]


def advanced(values, offset):
    if offset == 0:
        return values
    widths = [(0, 0)] * values.ndim
    widths[1] = (0, offset)
    return jnp.pad(values, widths)[:, offset:]


def space_sum(values):
    count = lax.axis_size("space")
    bits = _log2(count)
    if bits is None:
        return lax.psum(values, "space")
    for bit in range(bits):
        step = 1 << bit
        values = values + lax.ppermute(values, "space", [(i, i ^ step) for i in range(count)])
    return values


def _halve(cur, left, axis, bit, wire=None):
    size = lax.axis_size(axis)
    pos = left.index((axis, bit))
    hi, lo = 1 << pos, 1 << (len(left) - 1 - pos)
    mine = (lax.axis_index(axis) // (1 << bit)) % 2
    v = cur.reshape((hi, 2, lo) + cur.shape[1:])
    low, high = v[:, 0].reshape((hi * lo,) + cur.shape[1:]), v[:, 1].reshape((hi * lo,) + cur.shape[1:])
    upper = mine == 1
    keep = jnp.where(upper, high, low)
    send = jnp.where(upper, low, high)
    left.remove((axis, bit))
    if wire is not None:
        send = send.astype(wire)
    got = lax.ppermute(send, axis, [(i, i ^ (1 << bit)) for i in range(size)])
    return keep + got.astype(keep.dtype)


def halving_scatter(blocks, orders):
    nd, ns = lax.axis_size("dp"), lax.axis_size("space")
    bd, bs = _log2(nd), _log2(ns)
    if bd is None or bs is None:
        flat = lax.psum_scatter(blocks, "dp", scatter_dimension=0, tiled=True)
        return lax.psum_scatter(flat, "space", scatter_dimension=0, tiled=True)[0]
    natural = [("dp", i) for i in reversed(range(bd))] + [("space", i) for i in reversed(range(bs))]
    shared = 0
    while shared < len(natural) and all(o[shared] == orders[0][shared] for o in orders):
        shared += 1
    left = list(natural)
    cur = blocks
    for axis, bit in orders[0][:shared]:
        cur = _halve(cur, left, axis, bit)
    tail = len(natural)
    while tail > shared and all(o[tail - 1] == orders[0][tail - 1] for o in orders):
        tail -= 1
    width = cur.shape[1] // len(orders)
    outs = []
    for p, order in enumerate(orders):
        part, part_left = cur[:, p * width : (p + 1) * width], list(left)
        for axis, bit in order[shared:tail]:
            part = _halve(part, part_left, axis, bit, jnp.bfloat16)
        outs.append(part)
    cur = jnp.concatenate(outs, axis=1)
    for axis, bit in orders[0][tail:]:
        cur = _halve(cur, part_left, axis, bit)
    return cur[0]


def on_device(
    latents,
    lengths,
    spatial_weight,
    temporal_weight,
    critic_weight,
    critic_head,
    critic_frames,
    recon_grad,
):
    groups = lax.axis_size("space")
    devices = lax.axis_size("dp") * groups
    clip_count = latents.shape[0] * lax.axis_size("dp")
    frame_count = latents.shape[1]
    upsampled = upsample(latents)
    above, below = exchange_rows(latents, "space", 2)
    extended = jnp.concatenate(
        [upsample(above)[:, :, 1:], upsampled, upsample(below)[:, :, :1]], axis=2
    )
    padded = jnp.pad(extended, ((0, 0), (0, 0), (0, 0), (1, 1), (0, 0)))
    height = upsampled.shape[2]
    width = upsampled.shape[3]
    pre_act = jnp.zeros(upsampled.shape, jnp.float32)
    for row_tap in range(3):
        for col_tap in range(3):
            window = padded[:, :, row_tap : row_tap + height, col_tap : col_tap + width]
            pre_act = pre_act + jnp.einsum(
                "nfhwc,cd->nfhwd",
                window,
                spatial_weight[row_tap, col_tap],
                preferred_element_type=jnp.float32,
            )
    activated = jax.nn.silu(pre_act).astype(jnp.bfloat16)
    mixing = jnp.zeros(upsampled.shape, jnp.float32)
    for offset in range(3):
        mixing = mixing + jnp.einsum(
            "nfhwc,cd->nfhwd",
            delayed(activated, offset),
            temporal_weight[offset],
            preferred_element_type=jnp.float32,
        )
    alive_mask = (jnp.arange(frame_count)[None, :] < lengths[:, None]).astype(jnp.float32)[
        :, :, None, None, None
    ]
    decoded = (alive_mask * (upsampled.astype(jnp.float32) + mixing)).astype(jnp.bfloat16)
    chosen = jax.vmap(lambda clip_frames, indices: jnp.take(clip_frames, indices, axis=0))(
        decoded, critic_frames
    )
    hidden = jnp.einsum(
        "nqhwc,ce->nqhwe", chosen, critic_weight, preferred_element_type=jnp.float32
    )
    feature = space_sum(jnp.sum(jax.nn.gelu(hidden), axis=(2, 3))) / (height * groups * width)
    score_val = jnp.sum(feature * critic_head, axis=-1)
    factor = -jax.nn.sigmoid(-score_val)[..., None] * critic_head
    unused, pullback = jax.vjp(jax.nn.gelu, hidden)
    gelu_slope = pullback(jnp.broadcast_to(factor[..., None, None, :], hidden.shape))[0].astype(
        jnp.bfloat16
    )
    slope_rows = jnp.einsum(
        "nqhwe,ce->nqhwc", gelu_slope, critic_weight, preferred_element_type=jnp.float32
    )
    selector = (critic_frames[:, :, None] == jnp.arange(frame_count)[None, None, :]).astype(
        jnp.float32
    )
    adverse_frames = jnp.einsum(
        "nqf,nqhwc->nfhwc", selector, slope_rows, precision=lax.Precision.HIGHEST
    )
    loss_scale = 1.0 / math.sqrt(clip_count * frame_count * height * groups * width)
    cotangent = (
        alive_mask * loss_scale * (recon_grad.astype(jnp.float32) + adverse_frames)
    ).astype(jnp.bfloat16)
    temporal_grad = jnp.stack(
        [
            jnp.einsum(
                "nfhwc,nfhwd->cd",
                delayed(activated, offset),
                cotangent,
                preferred_element_type=jnp.float32,
            )
            for offset in range(3)
        ]
    )
    act_grad = jnp.zeros(upsampled.shape, jnp.float32)
    for offset in range(3):
        act_grad = act_grad + jnp.einsum(
            "nfhwd,cd->nfhwc",
            advanced(cotangent, offset),
            temporal_weight[offset],
            preferred_element_type=jnp.float32,
        )
    pre_slope = (act_grad * silu_slope(pre_act)).astype(jnp.bfloat16)
    tap_grads = []
    for row_tap in range(3):
        for col_tap in range(3):
            window = padded[:, :, row_tap : row_tap + height, col_tap : col_tap + width]
            tap_grads.append(
                jnp.einsum("nfhwc,nfhwd->cd", window, pre_slope, preferred_element_type=jnp.float32)
            )
    channels = spatial_weight.shape[-1]
    spatial_grad = jnp.stack(tap_grads).reshape(devices, -1, channels)
    temporal_grad = temporal_grad.reshape(devices, -1, channels)
    core, x_bit, y_bit = ("dp", 0), ("dp", 1), ("dp", 2)
    z_lo, z_hi = ("space", 0), ("space", 1)
    nd = lax.axis_size("dp")
    if nd == 8 and groups == 4:
        orders = ([core, x_bit, y_bit, z_lo, z_hi], [core, y_bit, x_bit, z_lo, z_hi])
    else:
        plain = [("dp", i) for i in range(nd.bit_length() - 1)]
        orders = (plain + [("space", i) for i in range(groups.bit_length() - 1)],)
    share = halving_scatter(jnp.concatenate([spatial_grad, temporal_grad], axis=1), orders)
    spatial_rows = spatial_grad.shape[1]
    return (decoded, share[:spatial_rows].reshape(-1), share[spatial_rows:].reshape(-1))


def solution(mesh):
    placed = (
        P("dp", None, "space", None, None),
        P("dp"),
        P(),
        P(),
        P(),
        P(),
        P("dp", None),
        P("dp", None, "space", None, None),
    )
    return jax.shard_map(
        on_device,
        mesh=mesh,
        in_specs=placed,
        out_specs=(P("dp", None, "space", None, None), P(("dp", "space")), P(("dp", "space"))),
        check_vma=False,
    )
```

```python
import math

import jax
import jax.numpy as jnp
from jax import lax
from jax.sharding import PartitionSpec as P


def _log2(n):
    b = n.bit_length() - 1
    return b if (1 << b) == n else None


def exchange_rows(cells, axis, dim):
    count = lax.axis_size(axis)
    ends = count - 1
    head = lax.slice_in_dim(cells, 0, 1, axis=dim)
    tail = lax.slice_in_dim(cells, cells.shape[dim] - 1, cells.shape[dim], axis=dim)
    above = lax.ppermute(tail, axis, [(i, i + 1) for i in range(ends)])
    below = lax.ppermute(head, axis, [(i + 1, i) for i in range(ends)])
    return above, below


def upsample(values):
    doubled = jnp.repeat(values, 2, axis=-3)
    return jnp.repeat(doubled, 2, axis=-2)


def silu_slope(pre_act):
    sigmoid_val = jax.nn.sigmoid(pre_act)
    return sigmoid_val * (1.0 + pre_act * (1.0 - sigmoid_val))


def delayed(values, offset):
    if offset == 0:
        return values
    widths = [(0, 0)] * values.ndim
    widths[1] = (offset, 0)
    return jnp.pad(values, widths)[:, : values.shape[1]]


def advanced(values, offset):
    if offset == 0:
        return values
    widths = [(0, 0)] * values.ndim
    widths[1] = (0, offset)
    return jnp.pad(values, widths)[:, offset:]


def space_sum(values):
    count = lax.axis_size("space")
    bits = _log2(count)
    if bits is None:
        return lax.psum(values, "space")
    for bit in range(bits):
        step = 1 << bit
        values = values + lax.ppermute(values, "space", [(i, i ^ step) for i in range(count)])
    return values


def _halve(cur, left, axis, bit, wire=None):
    size = lax.axis_size(axis)
    pos = left.index((axis, bit))
    hi, lo = 1 << pos, 1 << (len(left) - 1 - pos)
    mine = (lax.axis_index(axis) // (1 << bit)) % 2
    v = cur.reshape((hi, 2, lo) + cur.shape[1:])
    low, high = v[:, 0].reshape((hi * lo,) + cur.shape[1:]), v[:, 1].reshape((hi * lo,) + cur.shape[1:])
    upper = mine == 1
    keep = jnp.where(upper, high, low)
    send = jnp.where(upper, low, high)
    left.remove((axis, bit))
    if wire is not None:
        send = send.astype(wire)
    got = lax.ppermute(send, axis, [(i, i ^ (1 << bit)) for i in range(size)])
    return keep + got.astype(keep.dtype)


def halving_scatter(blocks, orders):
    nd, ns = lax.axis_size("dp"), lax.axis_size("space")
    bd, bs = _log2(nd), _log2(ns)
    if bd is None or bs is None:
        flat = lax.psum_scatter(blocks, "dp", scatter_dimension=0, tiled=True)
        return lax.psum_scatter(flat, "space", scatter_dimension=0, tiled=True)[0]
    natural = [("dp", i) for i in reversed(range(bd))] + [("space", i) for i in reversed(range(bs))]
    shared = 0
    while shared < len(natural) and all(o[shared] == orders[0][shared] for o in orders):
        shared += 1
    left = list(natural)
    cur = blocks
    for axis, bit in orders[0][:shared]:
        cur = _halve(cur, left, axis, bit)
    tail = len(natural)
    while tail > shared and all(o[tail - 1] == orders[0][tail - 1] for o in orders):
        tail -= 1
    width = cur.shape[1] // len(orders)
    outs = []
    for p, order in enumerate(orders):
        part, part_left = cur[:, p * width : (p + 1) * width], list(left)
        for axis, bit in order[shared:tail]:
            part = _halve(part, part_left, axis, bit, jnp.bfloat16)
        outs.append(part)
    cur = jnp.concatenate(outs, axis=1)
    rest = orders[0][tail:]
    if sorted(rest) == [("space", i) for i in range(bs)] and part_left == rest[::-1] == natural[bd:]:
        me = lax.axis_index("space")
        total = lax.dynamic_index_in_dim(cur, me, 0, keepdims=False)
        for shift in range(1, ns):
            send = lax.dynamic_index_in_dim(cur, (me + shift) % ns, 0, keepdims=False)
            total = total + lax.ppermute(send, "space", [(i, (i + shift) % ns) for i in range(ns)])
        return total
    for axis, bit in rest:
        cur = _halve(cur, part_left, axis, bit)
    return cur[0]


def on_device(
    latents,
    lengths,
    spatial_weight,
    temporal_weight,
    critic_weight,
    critic_head,
    critic_frames,
    recon_grad,
):
    groups = lax.axis_size("space")
    devices = lax.axis_size("dp") * groups
    clip_count = latents.shape[0] * lax.axis_size("dp")
    frame_count = latents.shape[1]
    upsampled = upsample(latents)
    above, below = exchange_rows(latents, "space", 2)
    extended = jnp.concatenate(
        [upsample(above)[:, :, 1:], upsampled, upsample(below)[:, :, :1]], axis=2
    )
    padded = jnp.pad(extended, ((0, 0), (0, 0), (0, 0), (1, 1), (0, 0)))
    height = upsampled.shape[2]
    width = upsampled.shape[3]
    pre_act = jnp.zeros(upsampled.shape, jnp.float32)
    for row_tap in range(3):
        for col_tap in range(3):
            window = padded[:, :, row_tap : row_tap + height, col_tap : col_tap + width]
            pre_act = pre_act + jnp.einsum(
                "nfhwc,cd->nfhwd",
                window,
                spatial_weight[row_tap, col_tap],
                preferred_element_type=jnp.float32,
            )
    activated = jax.nn.silu(pre_act).astype(jnp.bfloat16)
    mixing = jnp.zeros(upsampled.shape, jnp.float32)
    for offset in range(3):
        mixing = mixing + jnp.einsum(
            "nfhwc,cd->nfhwd",
            delayed(activated, offset),
            temporal_weight[offset],
            preferred_element_type=jnp.float32,
        )
    alive_mask = (jnp.arange(frame_count)[None, :] < lengths[:, None]).astype(jnp.float32)[
        :, :, None, None, None
    ]
    decoded = (alive_mask * (upsampled.astype(jnp.float32) + mixing)).astype(jnp.bfloat16)
    chosen = jax.vmap(lambda clip_frames, indices: jnp.take(clip_frames, indices, axis=0))(
        decoded, critic_frames
    )
    hidden = jnp.einsum(
        "nqhwc,ce->nqhwe", chosen, critic_weight, preferred_element_type=jnp.float32
    )
    feature = space_sum(jnp.sum(jax.nn.gelu(hidden), axis=(2, 3))) / (height * groups * width)
    score_val = jnp.sum(feature * critic_head, axis=-1)
    factor = -jax.nn.sigmoid(-score_val)[..., None] * critic_head
    unused, pullback = jax.vjp(jax.nn.gelu, hidden)
    gelu_slope = pullback(jnp.broadcast_to(factor[..., None, None, :], hidden.shape))[0].astype(
        jnp.bfloat16
    )
    slope_rows = jnp.einsum(
        "nqhwe,ce->nqhwc", gelu_slope, critic_weight, preferred_element_type=jnp.float32
    )
    selector = (critic_frames[:, :, None] == jnp.arange(frame_count)[None, None, :]).astype(
        jnp.float32
    )
    adverse_frames = jnp.einsum(
        "nqf,nqhwc->nfhwc", selector, slope_rows, precision=lax.Precision.HIGHEST
    )
    loss_scale = 1.0 / math.sqrt(clip_count * frame_count * height * groups * width)
    cotangent = (
        alive_mask * loss_scale * (recon_grad.astype(jnp.float32) + adverse_frames)
    ).astype(jnp.bfloat16)
    temporal_grad = jnp.stack(
        [
            jnp.einsum(
                "nfhwc,nfhwd->cd",
                delayed(activated, offset),
                cotangent,
                preferred_element_type=jnp.float32,
            )
            for offset in range(3)
        ]
    )
    act_grad = jnp.zeros(upsampled.shape, jnp.float32)
    for offset in range(3):
        act_grad = act_grad + jnp.einsum(
            "nfhwd,cd->nfhwc",
            advanced(cotangent, offset),
            temporal_weight[offset],
            preferred_element_type=jnp.float32,
        )
    pre_slope = (act_grad * silu_slope(pre_act)).astype(jnp.bfloat16)
    tap_grads = []
    for row_tap in range(3):
        for col_tap in range(3):
            window = padded[:, :, row_tap : row_tap + height, col_tap : col_tap + width]
            tap_grads.append(
                jnp.einsum("nfhwc,nfhwd->cd", window, pre_slope, preferred_element_type=jnp.float32)
            )
    channels = spatial_weight.shape[-1]
    spatial_grad = jnp.stack(tap_grads).reshape(devices, -1, channels)
    temporal_grad = temporal_grad.reshape(devices, -1, channels)
    core, x_bit, y_bit = ("dp", 0), ("dp", 1), ("dp", 2)
    z_lo, z_hi = ("space", 0), ("space", 1)
    nd = lax.axis_size("dp")
    if nd == 8 and groups == 4:
        orders = ([core, x_bit, y_bit, z_lo, z_hi], [core, y_bit, x_bit, z_lo, z_hi])
    else:
        plain = [("dp", i) for i in range(nd.bit_length() - 1)]
        orders = (plain + [("space", i) for i in range(groups.bit_length() - 1)],)
    share = halving_scatter(jnp.concatenate([spatial_grad, temporal_grad], axis=1), orders)
    spatial_rows = spatial_grad.shape[1]
    return (decoded, share[:spatial_rows].reshape(-1), share[spatial_rows:].reshape(-1))


def solution(mesh):
    placed = (
        P("dp", None, "space", None, None),
        P("dp"),
        P(),
        P(),
        P(),
        P(),
        P("dp", None),
        P("dp", None, "space", None, None),
    )
    return jax.shard_map(
        on_device,
        mesh=mesh,
        in_specs=placed,
        out_specs=(P("dp", None, "space", None, None), P(("dp", "space")), P(("dp", "space"))),
        check_vma=False,
    )
```

```python
import math

import jax
import jax.numpy as jnp
from jax import lax
from jax.sharding import PartitionSpec as P


def _log2(n):
    b = n.bit_length() - 1
    return b if (1 << b) == n else None


def exchange_rows(cells, axis, dim):
    count = lax.axis_size(axis)
    ends = count - 1
    head = lax.slice_in_dim(cells, 0, 1, axis=dim)
    tail = lax.slice_in_dim(cells, cells.shape[dim] - 1, cells.shape[dim], axis=dim)
    above = lax.ppermute(tail, axis, [(i, i + 1) for i in range(ends)])
    below = lax.ppermute(head, axis, [(i + 1, i) for i in range(ends)])
    return above, below


def upsample(values):
    doubled = jnp.repeat(values, 2, axis=-3)
    return jnp.repeat(doubled, 2, axis=-2)


def silu_slope(pre_act):
    sigmoid_val = jax.nn.sigmoid(pre_act)
    return sigmoid_val * (1.0 + pre_act * (1.0 - sigmoid_val))


def delayed(values, offset):
    if offset == 0:
        return values
    widths = [(0, 0)] * values.ndim
    widths[1] = (offset, 0)
    return jnp.pad(values, widths)[:, : values.shape[1]]


def advanced(values, offset):
    if offset == 0:
        return values
    widths = [(0, 0)] * values.ndim
    widths[1] = (0, offset)
    return jnp.pad(values, widths)[:, offset:]


def space_sum(values):
    count = lax.axis_size("space")
    bits = _log2(count)
    if bits is None:
        return lax.psum(values, "space")
    for bit in range(bits):
        step = 1 << bit
        values = values + lax.ppermute(values, "space", [(i, i ^ step) for i in range(count)])
    return values


def _halve(cur, left, axis, bit, wire=None):
    size = lax.axis_size(axis)
    pos = left.index((axis, bit))
    hi, lo = 1 << pos, 1 << (len(left) - 1 - pos)
    mine = (lax.axis_index(axis) // (1 << bit)) % 2
    v = cur.reshape((hi, 2, lo) + cur.shape[1:])
    low, high = v[:, 0].reshape((hi * lo,) + cur.shape[1:]), v[:, 1].reshape((hi * lo,) + cur.shape[1:])
    upper = mine == 1
    keep = jnp.where(upper, high, low)
    send = jnp.where(upper, low, high)
    left.remove((axis, bit))
    if wire is not None:
        send = send.astype(wire)
    got = lax.ppermute(send, axis, [(i, i ^ (1 << bit)) for i in range(size)])
    return keep + got.astype(keep.dtype)


def halving_scatter(blocks, orders):
    nd, ns = lax.axis_size("dp"), lax.axis_size("space")
    bd, bs = _log2(nd), _log2(ns)
    if bd is None or bs is None:
        flat = lax.psum_scatter(blocks, "dp", scatter_dimension=0, tiled=True)
        return [lax.psum_scatter(flat, "space", scatter_dimension=0, tiled=True)[0]]
    natural = [("dp", i) for i in reversed(range(bd))] + [("space", i) for i in reversed(range(bs))]
    shared = 0
    while shared < len(natural) and all(o[shared] == orders[0][shared] for o in orders):
        shared += 1
    left = list(natural)
    cur = blocks
    for axis, bit in orders[0][:shared]:
        cur = _halve(cur, left, axis, bit)
    tail = len(natural)
    while tail > shared and all(o[tail - 1] == orders[0][tail - 1] for o in orders):
        tail -= 1
    width = cur.shape[1] // len(orders)
    outs = []
    for p, order in enumerate(orders):
        part, part_left = cur[:, p * width : (p + 1) * width], list(left)
        for axis, bit in order[shared:tail]:
            part = _halve(part, part_left, axis, bit, jnp.bfloat16)
        outs.append(part)
    cur = jnp.concatenate(outs, axis=1)
    rest = orders[0][tail:]
    if sorted(rest) == [("space", i) for i in range(bs)] and part_left == rest[::-1] == natural[bd:]:
        me = lax.axis_index("space")
        terms = [lax.dynamic_index_in_dim(cur, me, 0, keepdims=False)]
        for shift in range(1, ns):
            send = lax.dynamic_index_in_dim(cur, (me + shift) % ns, 0, keepdims=False)
            terms.append(lax.ppermute(send, "space", [(i, (i + shift) % ns) for i in range(ns)]))
        return terms
    for axis, bit in rest:
        cur = _halve(cur, part_left, axis, bit)
    return [cur[0]]


def on_device(
    latents,
    lengths,
    spatial_weight,
    temporal_weight,
    critic_weight,
    critic_head,
    critic_frames,
    recon_grad,
):
    groups = lax.axis_size("space")
    devices = lax.axis_size("dp") * groups
    clip_count = latents.shape[0] * lax.axis_size("dp")
    frame_count = latents.shape[1]
    upsampled = upsample(latents)
    above, below = exchange_rows(latents, "space", 2)
    extended = jnp.concatenate(
        [upsample(above)[:, :, 1:], upsampled, upsample(below)[:, :, :1]], axis=2
    )
    padded = jnp.pad(extended, ((0, 0), (0, 0), (0, 0), (1, 1), (0, 0)))
    height = upsampled.shape[2]
    width = upsampled.shape[3]
    pre_act = jnp.zeros(upsampled.shape, jnp.float32)
    for row_tap in range(3):
        for col_tap in range(3):
            window = padded[:, :, row_tap : row_tap + height, col_tap : col_tap + width]
            pre_act = pre_act + jnp.einsum(
                "nfhwc,cd->nfhwd",
                window,
                spatial_weight[row_tap, col_tap],
                preferred_element_type=jnp.float32,
            )
    activated = jax.nn.silu(pre_act).astype(jnp.bfloat16)
    mixing = jnp.zeros(upsampled.shape, jnp.float32)
    for offset in range(3):
        mixing = mixing + jnp.einsum(
            "nfhwc,cd->nfhwd",
            delayed(activated, offset),
            temporal_weight[offset],
            preferred_element_type=jnp.float32,
        )
    alive_mask = (jnp.arange(frame_count)[None, :] < lengths[:, None]).astype(jnp.float32)[
        :, :, None, None, None
    ]
    decoded = (alive_mask * (upsampled.astype(jnp.float32) + mixing)).astype(jnp.bfloat16)
    picker = (critic_frames[:, :, None] == jnp.arange(frame_count)[None, None, :]).astype(
        jnp.bfloat16
    )
    chosen = jnp.einsum(
        "nqf,nfhwc->nqhwc", picker, decoded, preferred_element_type=jnp.float32
    ).astype(jnp.bfloat16)
    hidden = jnp.einsum(
        "nqhwc,ce->nqhwe", chosen, critic_weight, preferred_element_type=jnp.float32
    )
    feature = space_sum(jnp.sum(jax.nn.gelu(hidden), axis=(2, 3))) / (height * groups * width)
    score_val = jnp.sum(feature * critic_head, axis=-1)
    factor = -jax.nn.sigmoid(-score_val)[..., None] * critic_head
    unused, pullback = jax.vjp(jax.nn.gelu, hidden)
    gelu_slope = pullback(jnp.broadcast_to(factor[..., None, None, :], hidden.shape))[0].astype(
        jnp.bfloat16
    )
    slope_rows = jnp.einsum(
        "nqhwe,ce->nqhwc", gelu_slope, critic_weight, preferred_element_type=jnp.float32
    )
    selector = (critic_frames[:, :, None] == jnp.arange(frame_count)[None, None, :]).astype(
        jnp.float32
    )
    adverse_frames = jnp.einsum(
        "nqf,nqhwc->nfhwc", selector, slope_rows, precision=lax.Precision.HIGHEST
    )
    loss_scale = 1.0 / math.sqrt(clip_count * frame_count * height * groups * width)
    cotangent = (
        alive_mask * loss_scale * (recon_grad.astype(jnp.float32) + adverse_frames)
    ).astype(jnp.bfloat16)
    temporal_grad = jnp.stack(
        [
            jnp.einsum(
                "nfhwc,nfhwd->cd",
                delayed(activated, offset),
                cotangent,
                preferred_element_type=jnp.float32,
            )
            for offset in range(3)
        ]
    )
    act_grad = jnp.zeros(upsampled.shape, jnp.float32)
    for offset in range(3):
        act_grad = act_grad + jnp.einsum(
            "nfhwd,cd->nfhwc",
            advanced(cotangent, offset),
            temporal_weight[offset],
            preferred_element_type=jnp.float32,
        )
    pre_slope = (act_grad * silu_slope(pre_act)).astype(jnp.bfloat16)
    tap_grads = []
    for row_tap in range(3):
        for col_tap in range(3):
            window = padded[:, :, row_tap : row_tap + height, col_tap : col_tap + width]
            tap_grads.append(
                jnp.einsum("nfhwc,nfhwd->cd", window, pre_slope, preferred_element_type=jnp.float32)
            )
    channels = spatial_weight.shape[-1]
    spatial_grad = jnp.stack(tap_grads).reshape(devices, -1, channels)
    temporal_grad = temporal_grad.reshape(devices, -1, channels)
    core, x_bit, y_bit = ("dp", 0), ("dp", 1), ("dp", 2)
    z_lo, z_hi = ("space", 0), ("space", 1)
    nd = lax.axis_size("dp")
    if nd == 8 and groups == 4:
        orders = ([core, x_bit, y_bit, z_lo, z_hi], [core, y_bit, x_bit, z_lo, z_hi])
    else:
        plain = [("dp", i) for i in range(nd.bit_length() - 1)]
        orders = (plain + [("space", i) for i in range(groups.bit_length() - 1)],)
    share = halving_scatter(jnp.concatenate([spatial_grad, temporal_grad], axis=1), orders)
    spatial_rows = spatial_grad.shape[1]
    spatial_share = share[0][:spatial_rows].reshape(-1)
    temporal_share = share[0][spatial_rows:].reshape(-1)
    for term in share[1:]:
        spatial_share = spatial_share + term[:spatial_rows].reshape(-1)
        temporal_share = temporal_share + term[spatial_rows:].reshape(-1)
    return (decoded, spatial_share, temporal_share)


def solution(mesh):
    placed = (
        P("dp", None, "space", None, None),
        P("dp"),
        P(),
        P(),
        P(),
        P(),
        P("dp", None),
        P("dp", None, "space", None, None),
    )
    return jax.shard_map(
        on_device,
        mesh=mesh,
        in_specs=placed,
        out_specs=(P("dp", None, "space", None, None), P(("dp", "space")), P(("dp", "space"))),
        check_vma=False,
    )
```

```python
import math

import jax
import jax.numpy as jnp
from jax import lax
from jax.sharding import PartitionSpec as P


def _log2(n):
    b = n.bit_length() - 1
    return b if (1 << b) == n else None


def exchange_rows(cells, axis, dim):
    count = lax.axis_size(axis)
    ends = count - 1
    head = lax.slice_in_dim(cells, 0, 1, axis=dim)
    tail = lax.slice_in_dim(cells, cells.shape[dim] - 1, cells.shape[dim], axis=dim)
    above = lax.ppermute(tail, axis, [(i, i + 1) for i in range(ends)])
    below = lax.ppermute(head, axis, [(i + 1, i) for i in range(ends)])
    return above, below


def upsample(values):
    doubled = jnp.repeat(values, 2, axis=-3)
    return jnp.repeat(doubled, 2, axis=-2)


def silu_slope(pre_act):
    sigmoid_val = jax.nn.sigmoid(pre_act)
    return sigmoid_val * (1.0 + pre_act * (1.0 - sigmoid_val))


def delayed(values, offset):
    if offset == 0:
        return values
    widths = [(0, 0)] * values.ndim
    widths[1] = (offset, 0)
    return jnp.pad(values, widths)[:, : values.shape[1]]


def advanced(values, offset):
    if offset == 0:
        return values
    widths = [(0, 0)] * values.ndim
    widths[1] = (0, offset)
    return jnp.pad(values, widths)[:, offset:]


def space_sum(values):
    count = lax.axis_size("space")
    bits = _log2(count)
    if bits is None:
        return lax.psum(values, "space")
    for bit in range(bits):
        step = 1 << bit
        values = values + lax.ppermute(values, "space", [(i, i ^ step) for i in range(count)])
    return values


def _halve(cur, left, axis, bit, wire=None):
    size = lax.axis_size(axis)
    pos = left.index((axis, bit))
    hi, lo = 1 << pos, 1 << (len(left) - 1 - pos)
    mine = (lax.axis_index(axis) // (1 << bit)) % 2
    v = cur.reshape((hi, 2, lo) + cur.shape[1:])
    low, high = v[:, 0].reshape((hi * lo,) + cur.shape[1:]), v[:, 1].reshape((hi * lo,) + cur.shape[1:])
    upper = mine == 1
    keep = jnp.where(upper, high, low)
    send = jnp.where(upper, low, high)
    left.remove((axis, bit))
    if wire is not None:
        send = send.astype(wire)
    got = lax.ppermute(send, axis, [(i, i ^ (1 << bit)) for i in range(size)])
    return keep + got.astype(keep.dtype)


def halving_scatter(blocks, orders):
    nd, ns = lax.axis_size("dp"), lax.axis_size("space")
    bd, bs = _log2(nd), _log2(ns)
    if bd is None or bs is None:
        flat = lax.psum_scatter(blocks, "dp", scatter_dimension=0, tiled=True)
        return [lax.psum_scatter(flat, "space", scatter_dimension=0, tiled=True)[0]]
    natural = [("dp", i) for i in reversed(range(bd))] + [("space", i) for i in reversed(range(bs))]
    shared = 0
    while shared < len(natural) and all(o[shared] == orders[0][shared] for o in orders):
        shared += 1
    left = list(natural)
    cur = blocks
    for axis, bit in orders[0][:shared]:
        cur = _halve(cur, left, axis, bit)
    tail = len(natural)
    while tail > shared and all(o[tail - 1] == orders[0][tail - 1] for o in orders):
        tail -= 1
    width = cur.shape[1] // len(orders)
    outs = []
    for p, order in enumerate(orders):
        part, part_left = cur[:, p * width : (p + 1) * width], list(left)
        for axis, bit in order[shared:tail]:
            part = _halve(part, part_left, axis, bit, jnp.bfloat16)
        outs.append(part)
    cur = jnp.concatenate(outs, axis=1)
    rest = orders[0][tail:]
    if sorted(rest) == [("space", i) for i in range(bs)] and part_left == rest[::-1] == natural[bd:]:
        me = lax.axis_index("space")
        terms = [lax.dynamic_index_in_dim(cur, me, 0, keepdims=False)]
        for shift in range(1, ns):
            send = lax.dynamic_index_in_dim(cur, (me + shift) % ns, 0, keepdims=False)
            terms.append(lax.ppermute(send, "space", [(i, (i + shift) % ns) for i in range(ns)]))
        return terms
    for axis, bit in rest:
        cur = _halve(cur, part_left, axis, bit)
    return [cur[0]]


def on_device(
    latents,
    lengths,
    spatial_weight,
    temporal_weight,
    critic_weight,
    critic_head,
    critic_frames,
    recon_grad,
):
    groups = lax.axis_size("space")
    devices = lax.axis_size("dp") * groups
    clip_count = latents.shape[0] * lax.axis_size("dp")
    frame_count = latents.shape[1]
    upsampled = upsample(latents)
    height = upsampled.shape[2]
    width = upsampled.shape[3]
    own = jnp.pad(upsampled, ((0, 0), (0, 0), (1, 1), (1, 1), (0, 0)))
    local = jnp.zeros(upsampled.shape, jnp.float32)
    for row_tap in range(3):
        for col_tap in range(3):
            window = own[:, :, row_tap : row_tap + height, col_tap : col_tap + width]
            local = local + jnp.einsum(
                "nfhwc,cd->nfhwd",
                window,
                spatial_weight[row_tap, col_tap],
                preferred_element_type=jnp.float32,
            )
    local, ready = lax.optimization_barrier((local, latents))
    above, below = exchange_rows(ready, "space", 2)
    above_row = jnp.pad(upsample(above)[:, :, 1:], ((0, 0), (0, 0), (0, 0), (1, 1), (0, 0)))
    below_row = jnp.pad(upsample(below)[:, :, :1], ((0, 0), (0, 0), (0, 0), (1, 1), (0, 0)))
    top = jnp.zeros(above_row.shape[:3] + (width, local.shape[-1]), jnp.float32)
    bottom = jnp.zeros(top.shape, jnp.float32)
    for col_tap in range(3):
        top = top + jnp.einsum(
            "nfhwc,cd->nfhwd",
            above_row[:, :, :, col_tap : col_tap + width],
            spatial_weight[0, col_tap],
            preferred_element_type=jnp.float32,
        )
        bottom = bottom + jnp.einsum(
            "nfhwc,cd->nfhwd",
            below_row[:, :, :, col_tap : col_tap + width],
            spatial_weight[2, col_tap],
            preferred_element_type=jnp.float32,
        )
    edge = ((0, 0), (0, 0), (0, height - 1), (0, 0), (0, 0))
    pre_act = local + jnp.pad(top, edge) + jnp.pad(bottom, edge[:2] + ((height - 1, 0),) + edge[3:])
    padded = jnp.concatenate([above_row, own[:, :, 1:-1], below_row], axis=2)
    activated = jax.nn.silu(pre_act).astype(jnp.bfloat16)
    mixing = jnp.zeros(upsampled.shape, jnp.float32)
    for offset in range(3):
        mixing = mixing + jnp.einsum(
            "nfhwc,cd->nfhwd",
            delayed(activated, offset),
            temporal_weight[offset],
            preferred_element_type=jnp.float32,
        )
    alive_mask = (jnp.arange(frame_count)[None, :] < lengths[:, None]).astype(jnp.float32)[
        :, :, None, None, None
    ]
    decoded = (alive_mask * (upsampled.astype(jnp.float32) + mixing)).astype(jnp.bfloat16)
    picker = (critic_frames[:, :, None] == jnp.arange(frame_count)[None, None, :]).astype(
        jnp.bfloat16
    )
    chosen = jnp.einsum(
        "nqf,nfhwc->nqhwc", picker, decoded, preferred_element_type=jnp.float32
    ).astype(jnp.bfloat16)
    hidden = jnp.einsum(
        "nqhwc,ce->nqhwe", chosen, critic_weight, preferred_element_type=jnp.float32
    )
    feature = space_sum(jnp.sum(jax.nn.gelu(hidden), axis=(2, 3))) / (height * groups * width)
    score_val = jnp.sum(feature * critic_head, axis=-1)
    factor = -jax.nn.sigmoid(-score_val)[..., None] * critic_head
    unused, pullback = jax.vjp(jax.nn.gelu, hidden)
    gelu_slope = pullback(jnp.broadcast_to(factor[..., None, None, :], hidden.shape))[0].astype(
        jnp.bfloat16
    )
    slope_rows = jnp.einsum(
        "nqhwe,ce->nqhwc", gelu_slope, critic_weight, preferred_element_type=jnp.float32
    )
    selector = (critic_frames[:, :, None] == jnp.arange(frame_count)[None, None, :]).astype(
        jnp.float32
    )
    adverse_frames = jnp.einsum(
        "nqf,nqhwc->nfhwc", selector, slope_rows, precision=lax.Precision.HIGHEST
    )
    loss_scale = 1.0 / math.sqrt(clip_count * frame_count * height * groups * width)
    cotangent = (
        alive_mask * loss_scale * (recon_grad.astype(jnp.float32) + adverse_frames)
    ).astype(jnp.bfloat16)
    temporal_grad = jnp.stack(
        [
            jnp.einsum(
                "nfhwc,nfhwd->cd",
                delayed(activated, offset),
                cotangent,
                preferred_element_type=jnp.float32,
            )
            for offset in range(3)
        ]
    )
    act_grad = jnp.zeros(upsampled.shape, jnp.float32)
    for offset in range(3):
        act_grad = act_grad + jnp.einsum(
            "nfhwd,cd->nfhwc",
            advanced(cotangent, offset),
            temporal_weight[offset],
            preferred_element_type=jnp.float32,
        )
    pre_slope = (act_grad * silu_slope(pre_act)).astype(jnp.bfloat16)
    tap_grads = []
    for row_tap in range(3):
        for col_tap in range(3):
            window = padded[:, :, row_tap : row_tap + height, col_tap : col_tap + width]
            tap_grads.append(
                jnp.einsum("nfhwc,nfhwd->cd", window, pre_slope, preferred_element_type=jnp.float32)
            )
    channels = spatial_weight.shape[-1]
    spatial_grad = jnp.stack(tap_grads).reshape(devices, -1, channels)
    temporal_grad = temporal_grad.reshape(devices, -1, channels)
    core, x_bit, y_bit = ("dp", 0), ("dp", 1), ("dp", 2)
    z_lo, z_hi = ("space", 0), ("space", 1)
    nd = lax.axis_size("dp")
    if nd == 8 and groups == 4:
        orders = ([core, x_bit, y_bit, z_lo, z_hi], [core, y_bit, x_bit, z_lo, z_hi])
    else:
        plain = [("dp", i) for i in range(nd.bit_length() - 1)]
        orders = (plain + [("space", i) for i in range(groups.bit_length() - 1)],)
    share = halving_scatter(jnp.concatenate([spatial_grad, temporal_grad], axis=1), orders)
    spatial_rows = spatial_grad.shape[1]
    spatial_share = share[0][:spatial_rows].reshape(-1)
    temporal_share = share[0][spatial_rows:].reshape(-1)
    for term in share[1:]:
        spatial_share = spatial_share + term[:spatial_rows].reshape(-1)
        temporal_share = temporal_share + term[spatial_rows:].reshape(-1)
    return (decoded, spatial_share, temporal_share)


def solution(mesh):
    placed = (
        P("dp", None, "space", None, None),
        P("dp"),
        P(),
        P(),
        P(),
        P(),
        P("dp", None),
        P("dp", None, "space", None, None),
    )
    return jax.shard_map(
        on_device,
        mesh=mesh,
        in_specs=placed,
        out_specs=(P("dp", None, "space", None, None), P(("dp", "space")), P(("dp", "space"))),
        check_vma=False,
    )
```

```python
import math

import jax
import jax.numpy as jnp
from jax import lax
from jax.sharding import PartitionSpec as P


def _log2(n):
    b = n.bit_length() - 1
    return b if (1 << b) == n else None


def exchange_rows(cells, axis, dim):
    count = lax.axis_size(axis)
    ends = count - 1
    head = lax.slice_in_dim(cells, 0, 1, axis=dim)
    tail = lax.slice_in_dim(cells, cells.shape[dim] - 1, cells.shape[dim], axis=dim)
    above = lax.ppermute(tail, axis, [(i, i + 1) for i in range(ends)])
    below = lax.ppermute(head, axis, [(i + 1, i) for i in range(ends)])
    return above, below


def upsample(values):
    doubled = jnp.repeat(values, 2, axis=-3)
    return jnp.repeat(doubled, 2, axis=-2)


def silu_slope(pre_act):
    sigmoid_val = jax.nn.sigmoid(pre_act)
    return sigmoid_val * (1.0 + pre_act * (1.0 - sigmoid_val))


def delayed(values, offset):
    if offset == 0:
        return values
    widths = [(0, 0)] * values.ndim
    widths[1] = (offset, 0)
    return jnp.pad(values, widths)[:, : values.shape[1]]


def advanced(values, offset):
    if offset == 0:
        return values
    widths = [(0, 0)] * values.ndim
    widths[1] = (0, offset)
    return jnp.pad(values, widths)[:, offset:]


def space_sum(values):
    count = lax.axis_size("space")
    if count > 4:
        return lax.psum(values, "space")
    me = lax.axis_index("space")
    terms = [values] + [
        lax.ppermute(values, "space", [(i, (i + shift) % count) for i in range(count)])
        for shift in range(1, count)
    ]
    stacked = jnp.stack(terms)
    ordered = jnp.take(stacked, (me - jnp.arange(count)) % count, axis=0)
    total = ordered[0]
    for t in range(1, count):
        total = total + ordered[t]
    return total


def _halve(cur, left, axis, bit, wire=None):
    size = lax.axis_size(axis)
    pos = left.index((axis, bit))
    hi, lo = 1 << pos, 1 << (len(left) - 1 - pos)
    mine = (lax.axis_index(axis) // (1 << bit)) % 2
    v = cur.reshape((hi, 2, lo) + cur.shape[1:])
    low, high = v[:, 0].reshape((hi * lo,) + cur.shape[1:]), v[:, 1].reshape((hi * lo,) + cur.shape[1:])
    upper = mine == 1
    keep = jnp.where(upper, high, low)
    send = jnp.where(upper, low, high)
    left.remove((axis, bit))
    if wire is not None:
        send = send.astype(wire)
    got = lax.ppermute(send, axis, [(i, i ^ (1 << bit)) for i in range(size)])
    return keep + got.astype(keep.dtype)


def halving_scatter(blocks, orders):
    nd, ns = lax.axis_size("dp"), lax.axis_size("space")
    bd, bs = _log2(nd), _log2(ns)
    if bd is None or bs is None:
        flat = lax.psum_scatter(blocks, "dp", scatter_dimension=0, tiled=True)
        return [lax.psum_scatter(flat, "space", scatter_dimension=0, tiled=True)[0]]
    natural = [("dp", i) for i in reversed(range(bd))] + [("space", i) for i in reversed(range(bs))]
    shared = 0
    while shared < len(natural) and all(o[shared] == orders[0][shared] for o in orders):
        shared += 1
    left = list(natural)
    cur = blocks
    for axis, bit in orders[0][:shared]:
        cur = _halve(cur, left, axis, bit)
    tail = len(natural)
    while tail > shared and all(o[tail - 1] == orders[0][tail - 1] for o in orders):
        tail -= 1
    width = cur.shape[1] // len(orders)
    outs = []
    for p, order in enumerate(orders):
        part, part_left = cur[:, p * width : (p + 1) * width], list(left)
        for axis, bit in order[shared:tail]:
            part = _halve(part, part_left, axis, bit, jnp.bfloat16)
        outs.append(part)
    cur = jnp.concatenate(outs, axis=1)
    rest = orders[0][tail:]
    if sorted(rest) == [("space", i) for i in range(bs)] and part_left == rest[::-1] == natural[bd:]:
        me = lax.axis_index("space")
        terms = [lax.dynamic_index_in_dim(cur, me, 0, keepdims=False)]
        for shift in range(1, ns):
            send = lax.dynamic_index_in_dim(cur, (me + shift) % ns, 0, keepdims=False)
            terms.append(lax.ppermute(send, "space", [(i, (i + shift) % ns) for i in range(ns)]))
        return terms
    for axis, bit in rest:
        cur = _halve(cur, part_left, axis, bit)
    return [cur[0]]


def on_device(
    latents,
    lengths,
    spatial_weight,
    temporal_weight,
    critic_weight,
    critic_head,
    critic_frames,
    recon_grad,
):
    groups = lax.axis_size("space")
    devices = lax.axis_size("dp") * groups
    clip_count = latents.shape[0] * lax.axis_size("dp")
    frame_count = latents.shape[1]
    upsampled = upsample(latents)
    above, below = exchange_rows(latents, "space", 2)
    extended = jnp.concatenate(
        [upsample(above)[:, :, 1:], upsampled, upsample(below)[:, :, :1]], axis=2
    )
    padded = jnp.pad(extended, ((0, 0), (0, 0), (0, 0), (1, 1), (0, 0)))
    height = upsampled.shape[2]
    width = upsampled.shape[3]
    pre_act = jnp.zeros(upsampled.shape, jnp.float32)
    for row_tap in range(3):
        for col_tap in range(3):
            window = padded[:, :, row_tap : row_tap + height, col_tap : col_tap + width]
            pre_act = pre_act + jnp.einsum(
                "nfhwc,cd->nfhwd",
                window,
                spatial_weight[row_tap, col_tap],
                preferred_element_type=jnp.float32,
            )
    activated = jax.nn.silu(pre_act).astype(jnp.bfloat16)
    mixing = jnp.zeros(upsampled.shape, jnp.float32)
    for offset in range(3):
        mixing = mixing + jnp.einsum(
            "nfhwc,cd->nfhwd",
            delayed(activated, offset),
            temporal_weight[offset],
            preferred_element_type=jnp.float32,
        )
    alive_mask = (jnp.arange(frame_count)[None, :] < lengths[:, None]).astype(jnp.float32)[
        :, :, None, None, None
    ]
    decoded = (alive_mask * (upsampled.astype(jnp.float32) + mixing)).astype(jnp.bfloat16)
    picker = (critic_frames[:, :, None] == jnp.arange(frame_count)[None, None, :]).astype(
        jnp.bfloat16
    )
    chosen = jnp.einsum(
        "nqf,nfhwc->nqhwc", picker, decoded, preferred_element_type=jnp.float32
    ).astype(jnp.bfloat16)
    hidden = jnp.einsum(
        "nqhwc,ce->nqhwe", chosen, critic_weight, preferred_element_type=jnp.float32
    )
    feature = space_sum(jnp.sum(jax.nn.gelu(hidden), axis=(2, 3))) / (height * groups * width)
    score_val = jnp.sum(feature * critic_head, axis=-1)
    factor = -jax.nn.sigmoid(-score_val)[..., None] * critic_head
    unused, pullback = jax.vjp(jax.nn.gelu, hidden)
    gelu_slope = pullback(jnp.broadcast_to(factor[..., None, None, :], hidden.shape))[0].astype(
        jnp.bfloat16
    )
    slope_rows = jnp.einsum(
        "nqhwe,ce->nqhwc", gelu_slope, critic_weight, preferred_element_type=jnp.float32
    )
    selector = (critic_frames[:, :, None] == jnp.arange(frame_count)[None, None, :]).astype(
        jnp.float32
    )
    adverse_frames = jnp.einsum(
        "nqf,nqhwc->nfhwc", selector, slope_rows, precision=lax.Precision.HIGHEST
    )
    loss_scale = 1.0 / math.sqrt(clip_count * frame_count * height * groups * width)
    cotangent = (
        alive_mask * loss_scale * (recon_grad.astype(jnp.float32) + adverse_frames)
    ).astype(jnp.bfloat16)
    temporal_grad = jnp.stack(
        [
            jnp.einsum(
                "nfhwc,nfhwd->cd",
                delayed(activated, offset),
                cotangent,
                preferred_element_type=jnp.float32,
            )
            for offset in range(3)
        ]
    )
    act_grad = jnp.zeros(upsampled.shape, jnp.float32)
    for offset in range(3):
        act_grad = act_grad + jnp.einsum(
            "nfhwd,cd->nfhwc",
            advanced(cotangent, offset),
            temporal_weight[offset],
            preferred_element_type=jnp.float32,
        )
    pre_slope = (act_grad * silu_slope(pre_act)).astype(jnp.bfloat16)
    tap_grads = []
    for row_tap in range(3):
        for col_tap in range(3):
            window = padded[:, :, row_tap : row_tap + height, col_tap : col_tap + width]
            tap_grads.append(
                jnp.einsum("nfhwc,nfhwd->cd", window, pre_slope, preferred_element_type=jnp.float32)
            )
    channels = spatial_weight.shape[-1]
    spatial_grad = jnp.stack(tap_grads).reshape(devices, -1, channels)
    temporal_grad = temporal_grad.reshape(devices, -1, channels)
    core, x_bit, y_bit = ("dp", 0), ("dp", 1), ("dp", 2)
    z_lo, z_hi = ("space", 0), ("space", 1)
    nd = lax.axis_size("dp")
    if nd == 8 and groups == 4:
        orders = ([core, x_bit, y_bit, z_lo, z_hi], [core, y_bit, x_bit, z_lo, z_hi])
    else:
        plain = [("dp", i) for i in range(nd.bit_length() - 1)]
        orders = (plain + [("space", i) for i in range(groups.bit_length() - 1)],)
    share = halving_scatter(jnp.concatenate([spatial_grad, temporal_grad], axis=1), orders)
    spatial_rows = spatial_grad.shape[1]
    spatial_share = share[0][:spatial_rows].reshape(-1)
    temporal_share = share[0][spatial_rows:].reshape(-1)
    for term in share[1:]:
        spatial_share = spatial_share + term[:spatial_rows].reshape(-1)
        temporal_share = temporal_share + term[spatial_rows:].reshape(-1)
    return (decoded, spatial_share, temporal_share)


def solution(mesh):
    placed = (
        P("dp", None, "space", None, None),
        P("dp"),
        P(),
        P(),
        P(),
        P(),
        P("dp", None),
        P("dp", None, "space", None, None),
    )
    return jax.shard_map(
        on_device,
        mesh=mesh,
        in_specs=placed,
        out_specs=(P("dp", None, "space", None, None), P(("dp", "space")), P(("dp", "space"))),
        check_vma=False,
    )
```

```python
import math

import jax
import jax.numpy as jnp
from jax import lax
from jax.sharding import PartitionSpec as P


def _log2(n):
    b = n.bit_length() - 1
    return b if (1 << b) == n else None


def exchange_rows(cells, axis, dim):
    count = lax.axis_size(axis)
    ends = count - 1
    head = lax.slice_in_dim(cells, 0, 1, axis=dim)
    tail = lax.slice_in_dim(cells, cells.shape[dim] - 1, cells.shape[dim], axis=dim)
    above = lax.ppermute(tail, axis, [(i, i + 1) for i in range(ends)])
    below = lax.ppermute(head, axis, [(i + 1, i) for i in range(ends)])
    return above, below


def upsample(values):
    doubled = jnp.repeat(values, 2, axis=-3)
    return jnp.repeat(doubled, 2, axis=-2)


def silu_slope(pre_act):
    sigmoid_val = jax.nn.sigmoid(pre_act)
    return sigmoid_val * (1.0 + pre_act * (1.0 - sigmoid_val))


def delayed(values, offset):
    if offset == 0:
        return values
    widths = [(0, 0)] * values.ndim
    widths[1] = (offset, 0)
    return jnp.pad(values, widths)[:, : values.shape[1]]


def advanced(values, offset):
    if offset == 0:
        return values
    widths = [(0, 0)] * values.ndim
    widths[1] = (0, offset)
    return jnp.pad(values, widths)[:, offset:]


def space_sum(values):
    count = lax.axis_size("space")
    bits = _log2(count)
    if bits is None:
        return lax.psum(values, "space")
    for bit in range(bits):
        step = 1 << bit
        values = values + lax.ppermute(values, "space", [(i, i ^ step) for i in range(count)])
    return values


def _halve(cur, left, axis, bit, wire=None):
    size = lax.axis_size(axis)
    pos = left.index((axis, bit))
    hi, lo = 1 << pos, 1 << (len(left) - 1 - pos)
    mine = (lax.axis_index(axis) // (1 << bit)) % 2
    v = cur.reshape((hi, 2, lo) + cur.shape[1:])
    low, high = v[:, 0].reshape((hi * lo,) + cur.shape[1:]), v[:, 1].reshape((hi * lo,) + cur.shape[1:])
    upper = mine == 1
    keep = jnp.where(upper, high, low)
    send = jnp.where(upper, low, high)
    left.remove((axis, bit))
    if wire is not None:
        send = send.astype(wire)
    got = lax.ppermute(send, axis, [(i, i ^ (1 << bit)) for i in range(size)])
    return keep + got.astype(keep.dtype)


def halving_scatter(blocks, orders):
    nd, ns = lax.axis_size("dp"), lax.axis_size("space")
    bd, bs = _log2(nd), _log2(ns)
    if bd is None or bs is None:
        flat = lax.psum_scatter(blocks, "dp", scatter_dimension=0, tiled=True)
        return [lax.psum_scatter(flat, "space", scatter_dimension=0, tiled=True)[0]]
    natural = [("dp", i) for i in reversed(range(bd))] + [("space", i) for i in reversed(range(bs))]
    shared = 0
    while shared < len(natural) and all(o[shared] == orders[0][shared] for o in orders):
        shared += 1
    left = list(natural)
    cur = blocks
    for axis, bit in orders[0][:shared]:
        cur = _halve(cur, left, axis, bit, jnp.bfloat16)
    tail = len(natural)
    while tail > shared and all(o[tail - 1] == orders[0][tail - 1] for o in orders):
        tail -= 1
    width = cur.shape[1] // len(orders)
    outs = []
    for p, order in enumerate(orders):
        part, part_left = cur[:, p * width : (p + 1) * width], list(left)
        for axis, bit in order[shared:tail]:
            part = _halve(part, part_left, axis, bit, jnp.bfloat16)
        outs.append(part)
    cur = jnp.concatenate(outs, axis=1)
    rest = orders[0][tail:]
    if sorted(rest) == [("space", i) for i in range(bs)] and part_left == rest[::-1] == natural[bd:]:
        me = lax.axis_index("space")
        terms = [lax.dynamic_index_in_dim(cur, me, 0, keepdims=False)]
        for shift in range(1, ns):
            send = lax.dynamic_index_in_dim(cur, (me + shift) % ns, 0, keepdims=False)
            terms.append(lax.ppermute(send, "space", [(i, (i + shift) % ns) for i in range(ns)]))
        return terms
    for axis, bit in rest:
        cur = _halve(cur, part_left, axis, bit)
    return [cur[0]]


def on_device(
    latents,
    lengths,
    spatial_weight,
    temporal_weight,
    critic_weight,
    critic_head,
    critic_frames,
    recon_grad,
):
    groups = lax.axis_size("space")
    devices = lax.axis_size("dp") * groups
    clip_count = latents.shape[0] * lax.axis_size("dp")
    frame_count = latents.shape[1]
    upsampled = upsample(latents)
    above, below = exchange_rows(latents, "space", 2)
    extended = jnp.concatenate(
        [upsample(above)[:, :, 1:], upsampled, upsample(below)[:, :, :1]], axis=2
    )
    padded = jnp.pad(extended, ((0, 0), (0, 0), (0, 0), (1, 1), (0, 0)))
    height = upsampled.shape[2]
    width = upsampled.shape[3]
    pre_act = jnp.zeros(upsampled.shape, jnp.float32)
    for row_tap in range(3):
        for col_tap in range(3):
            window = padded[:, :, row_tap : row_tap + height, col_tap : col_tap + width]
            pre_act = pre_act + jnp.einsum(
                "nfhwc,cd->nfhwd",
                window,
                spatial_weight[row_tap, col_tap],
                preferred_element_type=jnp.float32,
            )
    activated = jax.nn.silu(pre_act).astype(jnp.bfloat16)
    mixing = jnp.zeros(upsampled.shape, jnp.float32)
    for offset in range(3):
        mixing = mixing + jnp.einsum(
            "nfhwc,cd->nfhwd",
            delayed(activated, offset),
            temporal_weight[offset],
            preferred_element_type=jnp.float32,
        )
    alive_mask = (jnp.arange(frame_count)[None, :] < lengths[:, None]).astype(jnp.float32)[
        :, :, None, None, None
    ]
    decoded = (alive_mask * (upsampled.astype(jnp.float32) + mixing)).astype(jnp.bfloat16)
    picker = (critic_frames[:, :, None] == jnp.arange(frame_count)[None, None, :]).astype(
        jnp.bfloat16
    )
    chosen = jnp.einsum(
        "nqf,nfhwc->nqhwc", picker, decoded, preferred_element_type=jnp.float32
    ).astype(jnp.bfloat16)
    hidden = jnp.einsum(
        "nqhwc,ce->nqhwe", chosen, critic_weight, preferred_element_type=jnp.float32
    )
    feature = space_sum(jnp.sum(jax.nn.gelu(hidden), axis=(2, 3))) / (height * groups * width)
    score_val = jnp.sum(feature * critic_head, axis=-1)
    factor = -jax.nn.sigmoid(-score_val)[..., None] * critic_head
    unused, pullback = jax.vjp(jax.nn.gelu, hidden)
    gelu_slope = pullback(jnp.broadcast_to(factor[..., None, None, :], hidden.shape))[0].astype(
        jnp.bfloat16
    )
    slope_rows = jnp.einsum(
        "nqhwe,ce->nqhwc", gelu_slope, critic_weight, preferred_element_type=jnp.float32
    )
    selector = (critic_frames[:, :, None] == jnp.arange(frame_count)[None, None, :]).astype(
        jnp.float32
    )
    adverse_frames = jnp.einsum(
        "nqf,nqhwc->nfhwc", selector, slope_rows, precision=lax.Precision.HIGHEST
    )
    loss_scale = 1.0 / math.sqrt(clip_count * frame_count * height * groups * width)
    cotangent = (
        alive_mask * loss_scale * (recon_grad.astype(jnp.float32) + adverse_frames)
    ).astype(jnp.bfloat16)
    temporal_grad = jnp.stack(
        [
            jnp.einsum(
                "nfhwc,nfhwd->cd",
                delayed(activated, offset),
                cotangent,
                preferred_element_type=jnp.float32,
            )
            for offset in range(3)
        ]
    )
    act_grad = jnp.zeros(upsampled.shape, jnp.float32)
    for offset in range(3):
        act_grad = act_grad + jnp.einsum(
            "nfhwd,cd->nfhwc",
            advanced(cotangent, offset),
            temporal_weight[offset],
            preferred_element_type=jnp.float32,
        )
    pre_slope = (act_grad * silu_slope(pre_act)).astype(jnp.bfloat16)
    tap_grads = []
    for row_tap in range(3):
        for col_tap in range(3):
            window = padded[:, :, row_tap : row_tap + height, col_tap : col_tap + width]
            tap_grads.append(
                jnp.einsum("nfhwc,nfhwd->cd", window, pre_slope, preferred_element_type=jnp.float32)
            )
    channels = spatial_weight.shape[-1]
    spatial_grad = jnp.stack(tap_grads).reshape(devices, -1, channels)
    temporal_grad = temporal_grad.reshape(devices, -1, channels)
    core, x_bit, y_bit = ("dp", 0), ("dp", 1), ("dp", 2)
    z_lo, z_hi = ("space", 0), ("space", 1)
    nd = lax.axis_size("dp")
    if nd == 8 and groups == 4:
        orders = ([core, x_bit, y_bit, z_lo, z_hi], [core, y_bit, x_bit, z_lo, z_hi])
    else:
        plain = [("dp", i) for i in range(nd.bit_length() - 1)]
        orders = (plain + [("space", i) for i in range(groups.bit_length() - 1)],)
    share = halving_scatter(jnp.concatenate([spatial_grad, temporal_grad], axis=1), orders)
    spatial_rows = spatial_grad.shape[1]
    spatial_share = share[0][:spatial_rows].reshape(-1)
    temporal_share = share[0][spatial_rows:].reshape(-1)
    for term in share[1:]:
        spatial_share = spatial_share + term[:spatial_rows].reshape(-1)
        temporal_share = temporal_share + term[spatial_rows:].reshape(-1)
    return (decoded, spatial_share, temporal_share)


def solution(mesh):
    placed = (
        P("dp", None, "space", None, None),
        P("dp"),
        P(),
        P(),
        P(),
        P(),
        P("dp", None),
        P("dp", None, "space", None, None),
    )
    return jax.shard_map(
        on_device,
        mesh=mesh,
        in_specs=placed,
        out_specs=(P("dp", None, "space", None, None), P(("dp", "space")), P(("dp", "space"))),
        check_vma=False,
    )
```

```python
import math

import jax
import jax.numpy as jnp
from jax import lax
from jax.sharding import PartitionSpec as P


def _log2(n):
    b = n.bit_length() - 1
    return b if (1 << b) == n else None


def exchange_rows(cells, axis, dim):
    count = lax.axis_size(axis)
    me = lax.axis_index(axis)
    head = lax.slice_in_dim(cells, 0, 1, axis=dim)
    tail = lax.slice_in_dim(cells, cells.shape[dim] - 1, cells.shape[dim], axis=dim)
    above = lax.ppermute(tail, axis, [(i, (i + 1) % count) for i in range(count)])
    below = lax.ppermute(head, axis, [((i + 1) % count, i) for i in range(count)])
    above = jnp.where(me == 0, jnp.zeros_like(above), above)
    below = jnp.where(me == count - 1, jnp.zeros_like(below), below)
    return above, below


def upsample(values):
    doubled = jnp.repeat(values, 2, axis=-3)
    return jnp.repeat(doubled, 2, axis=-2)


def silu_slope(pre_act):
    sigmoid_val = jax.nn.sigmoid(pre_act)
    return sigmoid_val * (1.0 + pre_act * (1.0 - sigmoid_val))


def delayed(values, offset):
    if offset == 0:
        return values
    widths = [(0, 0)] * values.ndim
    widths[1] = (offset, 0)
    return jnp.pad(values, widths)[:, : values.shape[1]]


def advanced(values, offset):
    if offset == 0:
        return values
    widths = [(0, 0)] * values.ndim
    widths[1] = (0, offset)
    return jnp.pad(values, widths)[:, offset:]


def space_sum(values):
    count = lax.axis_size("space")
    bits = _log2(count)
    if bits is None:
        return lax.psum(values, "space")
    for bit in range(bits):
        step = 1 << bit
        values = values + lax.ppermute(values, "space", [(i, i ^ step) for i in range(count)])
    return values


def _halve(cur, left, axis, bit, wire=None):
    size = lax.axis_size(axis)
    pos = left.index((axis, bit))
    hi, lo = 1 << pos, 1 << (len(left) - 1 - pos)
    mine = (lax.axis_index(axis) // (1 << bit)) % 2
    v = cur.reshape((hi, 2, lo) + cur.shape[1:])
    low, high = v[:, 0].reshape((hi * lo,) + cur.shape[1:]), v[:, 1].reshape((hi * lo,) + cur.shape[1:])
    upper = mine == 1
    keep = jnp.where(upper, high, low)
    send = jnp.where(upper, low, high)
    left.remove((axis, bit))
    if wire is not None:
        send = send.astype(wire)
    got = lax.ppermute(send, axis, [(i, i ^ (1 << bit)) for i in range(size)])
    return keep + got.astype(keep.dtype)


def halving_scatter(blocks, orders):
    nd, ns = lax.axis_size("dp"), lax.axis_size("space")
    bd, bs = _log2(nd), _log2(ns)
    if bd is None or bs is None:
        flat = lax.psum_scatter(blocks, "dp", scatter_dimension=0, tiled=True)
        return [lax.psum_scatter(flat, "space", scatter_dimension=0, tiled=True)[0]]
    natural = [("dp", i) for i in reversed(range(bd))] + [("space", i) for i in reversed(range(bs))]
    shared = 0
    while shared < len(natural) and all(o[shared] == orders[0][shared] for o in orders):
        shared += 1
    left = list(natural)
    cur = blocks
    for axis, bit in orders[0][:shared]:
        cur = _halve(cur, left, axis, bit, jnp.bfloat16)
    tail = len(natural)
    while tail > shared and all(o[tail - 1] == orders[0][tail - 1] for o in orders):
        tail -= 1
    width = cur.shape[1] // len(orders)
    outs = []
    for p, order in enumerate(orders):
        part, part_left = cur[:, p * width : (p + 1) * width], list(left)
        for axis, bit in order[shared:tail]:
            part = _halve(part, part_left, axis, bit, jnp.bfloat16)
        outs.append(part)
    cur = jnp.concatenate(outs, axis=1)
    rest = orders[0][tail:]
    if sorted(rest) == [("space", i) for i in range(bs)] and part_left == rest[::-1] == natural[bd:]:
        me = lax.axis_index("space")
        terms = [lax.dynamic_index_in_dim(cur, me, 0, keepdims=False)]
        for shift in range(1, ns):
            send = lax.dynamic_index_in_dim(cur, (me + shift) % ns, 0, keepdims=False)
            terms.append(lax.ppermute(send, "space", [(i, (i + shift) % ns) for i in range(ns)]))
        return terms
    for axis, bit in rest:
        cur = _halve(cur, part_left, axis, bit)
    return [cur[0]]


def on_device(
    latents,
    lengths,
    spatial_weight,
    temporal_weight,
    critic_weight,
    critic_head,
    critic_frames,
    recon_grad,
):
    groups = lax.axis_size("space")
    devices = lax.axis_size("dp") * groups
    clip_count = latents.shape[0] * lax.axis_size("dp")
    frame_count = latents.shape[1]
    upsampled = upsample(latents)
    above, below = exchange_rows(latents, "space", 2)
    extended = jnp.concatenate(
        [upsample(above)[:, :, 1:], upsampled, upsample(below)[:, :, :1]], axis=2
    )
    padded = jnp.pad(extended, ((0, 0), (0, 0), (0, 0), (1, 1), (0, 0)))
    height = upsampled.shape[2]
    width = upsampled.shape[3]
    pre_act = jnp.zeros(upsampled.shape, jnp.float32)
    for row_tap in range(3):
        for col_tap in range(3):
            window = padded[:, :, row_tap : row_tap + height, col_tap : col_tap + width]
            pre_act = pre_act + jnp.einsum(
                "nfhwc,cd->nfhwd",
                window,
                spatial_weight[row_tap, col_tap],
                preferred_element_type=jnp.float32,
            )
    activated = jax.nn.silu(pre_act).astype(jnp.bfloat16)
    mixing = jnp.zeros(upsampled.shape, jnp.float32)
    for offset in range(3):
        mixing = mixing + jnp.einsum(
            "nfhwc,cd->nfhwd",
            delayed(activated, offset),
            temporal_weight[offset],
            preferred_element_type=jnp.float32,
        )
    alive_mask = (jnp.arange(frame_count)[None, :] < lengths[:, None]).astype(jnp.float32)[
        :, :, None, None, None
    ]
    decoded = (alive_mask * (upsampled.astype(jnp.float32) + mixing)).astype(jnp.bfloat16)
    picker = (critic_frames[:, :, None] == jnp.arange(frame_count)[None, None, :]).astype(
        jnp.bfloat16
    )
    chosen = jnp.einsum(
        "nqf,nfhwc->nqhwc", picker, decoded, preferred_element_type=jnp.float32
    ).astype(jnp.bfloat16)
    hidden = jnp.einsum(
        "nqhwc,ce->nqhwe", chosen, critic_weight, preferred_element_type=jnp.float32
    )
    feature = space_sum(jnp.sum(jax.nn.gelu(hidden), axis=(2, 3))) / (height * groups * width)
    score_val = jnp.sum(feature * critic_head, axis=-1)
    factor = -jax.nn.sigmoid(-score_val)[..., None] * critic_head
    unused, pullback = jax.vjp(jax.nn.gelu, hidden)
    gelu_slope = pullback(jnp.broadcast_to(factor[..., None, None, :], hidden.shape))[0].astype(
        jnp.bfloat16
    )
    slope_rows = jnp.einsum(
        "nqhwe,ce->nqhwc", gelu_slope, critic_weight, preferred_element_type=jnp.float32
    )
    selector = (critic_frames[:, :, None] == jnp.arange(frame_count)[None, None, :]).astype(
        jnp.float32
    )
    adverse_frames = jnp.einsum(
        "nqf,nqhwc->nfhwc", selector, slope_rows, precision=lax.Precision.HIGHEST
    )
    loss_scale = 1.0 / math.sqrt(clip_count * frame_count * height * groups * width)
    cotangent = (
        alive_mask * loss_scale * (recon_grad.astype(jnp.float32) + adverse_frames)
    ).astype(jnp.bfloat16)
    temporal_grad = jnp.stack(
        [
            jnp.einsum(
                "nfhwc,nfhwd->cd",
                delayed(activated, offset),
                cotangent,
                preferred_element_type=jnp.float32,
            )
            for offset in range(3)
        ]
    )
    act_grad = jnp.zeros(upsampled.shape, jnp.float32)
    for offset in range(3):
        act_grad = act_grad + jnp.einsum(
            "nfhwd,cd->nfhwc",
            advanced(cotangent, offset),
            temporal_weight[offset],
            preferred_element_type=jnp.float32,
        )
    pre_slope = (act_grad * silu_slope(pre_act)).astype(jnp.bfloat16)
    tap_grads = []
    for row_tap in range(3):
        for col_tap in range(3):
            window = padded[:, :, row_tap : row_tap + height, col_tap : col_tap + width]
            tap_grads.append(
                jnp.einsum("nfhwc,nfhwd->cd", window, pre_slope, preferred_element_type=jnp.float32)
            )
    channels = spatial_weight.shape[-1]
    spatial_grad = jnp.stack(tap_grads).reshape(devices, -1, channels)
    temporal_grad = temporal_grad.reshape(devices, -1, channels)
    core, x_bit, y_bit = ("dp", 0), ("dp", 1), ("dp", 2)
    z_lo, z_hi = ("space", 0), ("space", 1)
    nd = lax.axis_size("dp")
    if nd == 8 and groups == 4:
        orders = ([core, x_bit, y_bit, z_lo, z_hi], [core, y_bit, x_bit, z_lo, z_hi])
    else:
        plain = [("dp", i) for i in range(nd.bit_length() - 1)]
        orders = (plain + [("space", i) for i in range(groups.bit_length() - 1)],)
    share = halving_scatter(jnp.concatenate([spatial_grad, temporal_grad], axis=1), orders)
    spatial_rows = spatial_grad.shape[1]
    spatial_share = share[0][:spatial_rows].reshape(-1)
    temporal_share = share[0][spatial_rows:].reshape(-1)
    for term in share[1:]:
        spatial_share = spatial_share + term[:spatial_rows].reshape(-1)
        temporal_share = temporal_share + term[spatial_rows:].reshape(-1)
    return (decoded, spatial_share, temporal_share)


def solution(mesh):
    placed = (
        P("dp", None, "space", None, None),
        P("dp"),
        P(),
        P(),
        P(),
        P(),
        P("dp", None),
        P("dp", None, "space", None, None),
    )
    return jax.shard_map(
        on_device,
        mesh=mesh,
        in_specs=placed,
        out_specs=(P("dp", None, "space", None, None), P(("dp", "space")), P(("dp", "space"))),
        check_vma=False,
    )
```

```python
import math

import jax
import jax.numpy as jnp
from jax import lax
from jax.sharding import PartitionSpec as P


def _log2(n):
    b = n.bit_length() - 1
    return b if (1 << b) == n else None


def exchange_rows(cells, axis, dim):
    count = lax.axis_size(axis)
    ends = count - 1
    head = lax.slice_in_dim(cells, 0, 1, axis=dim)
    tail = lax.slice_in_dim(cells, cells.shape[dim] - 1, cells.shape[dim], axis=dim)
    above = lax.ppermute(tail, axis, [(i, i + 1) for i in range(ends)])
    below = lax.ppermute(head, axis, [(i + 1, i) for i in range(ends)])
    return above, below


def upsample(values):
    doubled = jnp.repeat(values, 2, axis=-3)
    return jnp.repeat(doubled, 2, axis=-2)


def silu_slope(pre_act):
    sigmoid_val = jax.nn.sigmoid(pre_act)
    return sigmoid_val * (1.0 + pre_act * (1.0 - sigmoid_val))


def delayed(values, offset):
    if offset == 0:
        return values
    widths = [(0, 0)] * values.ndim
    widths[1] = (offset, 0)
    return jnp.pad(values, widths)[:, : values.shape[1]]


def advanced(values, offset):
    if offset == 0:
        return values
    widths = [(0, 0)] * values.ndim
    widths[1] = (0, offset)
    return jnp.pad(values, widths)[:, offset:]


def space_sum(values):
    count = lax.axis_size("space")
    bits = _log2(count)
    if bits is None:
        return lax.psum(values, "space")
    for bit in range(bits):
        step = 1 << bit
        values = values + lax.ppermute(values, "space", [(i, i ^ step) for i in range(count)])
    return values


def _halve(cur, left, axis, bit, wire=None):
    size = lax.axis_size(axis)
    pos = left.index((axis, bit))
    hi, lo = 1 << pos, 1 << (len(left) - 1 - pos)
    mine = (lax.axis_index(axis) // (1 << bit)) % 2
    v = cur.reshape((hi, 2, lo) + cur.shape[1:])
    low, high = v[:, 0].reshape((hi * lo,) + cur.shape[1:]), v[:, 1].reshape((hi * lo,) + cur.shape[1:])
    upper = mine == 1
    keep = jnp.where(upper, high, low)
    send = jnp.where(upper, low, high)
    left.remove((axis, bit))
    if wire is not None:
        send = send.astype(wire)
    got = lax.ppermute(send, axis, [(i, i ^ (1 << bit)) for i in range(size)])
    return keep + got.astype(keep.dtype)


def halving_scatter(blocks, orders):
    nd, ns = lax.axis_size("dp"), lax.axis_size("space")
    bd, bs = _log2(nd), _log2(ns)
    if bd is None or bs is None:
        flat = lax.psum_scatter(blocks, "dp", scatter_dimension=0, tiled=True)
        return [lax.psum_scatter(flat, "space", scatter_dimension=0, tiled=True)[0]]
    natural = [("dp", i) for i in reversed(range(bd))] + [("space", i) for i in reversed(range(bs))]
    shared = 0
    while shared < len(natural) and all(o[shared] == orders[0][shared] for o in orders):
        shared += 1
    left = list(natural)
    cur = blocks
    for axis, bit in orders[0][:shared]:
        cur = _halve(cur, left, axis, bit, jnp.bfloat16)
    tail = len(natural)
    while tail > shared and all(o[tail - 1] == orders[0][tail - 1] for o in orders):
        tail -= 1
    width = cur.shape[1] // len(orders)
    outs = []
    for p, order in enumerate(orders):
        part, part_left = cur[:, p * width : (p + 1) * width], list(left)
        for axis, bit in order[shared:tail]:
            part = _halve(part, part_left, axis, bit, jnp.bfloat16)
        outs.append(part)
    cur = jnp.concatenate(outs, axis=1)
    rest = orders[0][tail:]
    if sorted(rest) == [("space", i) for i in range(bs)] and part_left == rest[::-1] == natural[bd:]:
        me = lax.axis_index("space")
        terms = [lax.dynamic_index_in_dim(cur, me, 0, keepdims=False)]
        for shift in range(1, ns):
            send = lax.dynamic_index_in_dim(cur, (me + shift) % ns, 0, keepdims=False)
            got = lax.ppermute(send.astype(jnp.bfloat16), "space", [(i, (i + shift) % ns) for i in range(ns)])
            terms.append(got.astype(cur.dtype))
        return terms
    for axis, bit in rest:
        cur = _halve(cur, part_left, axis, bit)
    return [cur[0]]


def on_device(
    latents,
    lengths,
    spatial_weight,
    temporal_weight,
    critic_weight,
    critic_head,
    critic_frames,
    recon_grad,
):
    groups = lax.axis_size("space")
    devices = lax.axis_size("dp") * groups
    clip_count = latents.shape[0] * lax.axis_size("dp")
    frame_count = latents.shape[1]
    upsampled = upsample(latents)
    above, below = exchange_rows(latents, "space", 2)
    extended = jnp.concatenate(
        [upsample(above)[:, :, 1:], upsampled, upsample(below)[:, :, :1]], axis=2
    )
    padded = jnp.pad(extended, ((0, 0), (0, 0), (0, 0), (1, 1), (0, 0)))
    height = upsampled.shape[2]
    width = upsampled.shape[3]
    pre_act = jnp.zeros(upsampled.shape, jnp.float32)
    for row_tap in range(3):
        for col_tap in range(3):
            window = padded[:, :, row_tap : row_tap + height, col_tap : col_tap + width]
            pre_act = pre_act + jnp.einsum(
                "nfhwc,cd->nfhwd",
                window,
                spatial_weight[row_tap, col_tap],
                preferred_element_type=jnp.float32,
            )
    activated = jax.nn.silu(pre_act).astype(jnp.bfloat16)
    mixing = jnp.zeros(upsampled.shape, jnp.float32)
    for offset in range(3):
        mixing = mixing + jnp.einsum(
            "nfhwc,cd->nfhwd",
            delayed(activated, offset),
            temporal_weight[offset],
            preferred_element_type=jnp.float32,
        )
    alive_mask = (jnp.arange(frame_count)[None, :] < lengths[:, None]).astype(jnp.float32)[
        :, :, None, None, None
    ]
    decoded = (alive_mask * (upsampled.astype(jnp.float32) + mixing)).astype(jnp.bfloat16)
    picker = (critic_frames[:, :, None] == jnp.arange(frame_count)[None, None, :]).astype(
        jnp.bfloat16
    )
    chosen = jnp.einsum(
        "nqf,nfhwc->nqhwc", picker, decoded, preferred_element_type=jnp.float32
    ).astype(jnp.bfloat16)
    hidden = jnp.einsum(
        "nqhwc,ce->nqhwe", chosen, critic_weight, preferred_element_type=jnp.float32
    )
    feature = space_sum(jnp.sum(jax.nn.gelu(hidden), axis=(2, 3))) / (height * groups * width)
    score_val = jnp.sum(feature * critic_head, axis=-1)
    factor = -jax.nn.sigmoid(-score_val)[..., None] * critic_head
    unused, pullback = jax.vjp(jax.nn.gelu, hidden)
    gelu_slope = pullback(jnp.broadcast_to(factor[..., None, None, :], hidden.shape))[0].astype(
        jnp.bfloat16
    )
    slope_rows = jnp.einsum(
        "nqhwe,ce->nqhwc", gelu_slope, critic_weight, preferred_element_type=jnp.float32
    )
    selector = (critic_frames[:, :, None] == jnp.arange(frame_count)[None, None, :]).astype(
        jnp.float32
    )
    adverse_frames = jnp.einsum(
        "nqf,nqhwc->nfhwc", selector, slope_rows, precision=lax.Precision.HIGHEST
    )
    loss_scale = 1.0 / math.sqrt(clip_count * frame_count * height * groups * width)
    cotangent = (
        alive_mask * loss_scale * (recon_grad.astype(jnp.float32) + adverse_frames)
    ).astype(jnp.bfloat16)
    temporal_grad = jnp.stack(
        [
            jnp.einsum(
                "nfhwc,nfhwd->cd",
                delayed(activated, offset),
                cotangent,
                preferred_element_type=jnp.float32,
            )
            for offset in range(3)
        ]
    )
    act_grad = jnp.zeros(upsampled.shape, jnp.float32)
    for offset in range(3):
        act_grad = act_grad + jnp.einsum(
            "nfhwd,cd->nfhwc",
            advanced(cotangent, offset),
            temporal_weight[offset],
            preferred_element_type=jnp.float32,
        )
    pre_slope = (act_grad * silu_slope(pre_act)).astype(jnp.bfloat16)
    tap_grads = []
    for row_tap in range(3):
        for col_tap in range(3):
            window = padded[:, :, row_tap : row_tap + height, col_tap : col_tap + width]
            tap_grads.append(
                jnp.einsum("nfhwc,nfhwd->cd", window, pre_slope, preferred_element_type=jnp.float32)
            )
    channels = spatial_weight.shape[-1]
    spatial_grad = jnp.stack(tap_grads).reshape(devices, -1, channels)
    temporal_grad = temporal_grad.reshape(devices, -1, channels)
    core, x_bit, y_bit = ("dp", 0), ("dp", 1), ("dp", 2)
    z_lo, z_hi = ("space", 0), ("space", 1)
    nd = lax.axis_size("dp")
    if nd == 8 and groups == 4:
        orders = ([core, x_bit, y_bit, z_lo, z_hi], [core, y_bit, x_bit, z_lo, z_hi])
    else:
        plain = [("dp", i) for i in range(nd.bit_length() - 1)]
        orders = (plain + [("space", i) for i in range(groups.bit_length() - 1)],)
    share = halving_scatter(jnp.concatenate([spatial_grad, temporal_grad], axis=1), orders)
    spatial_rows = spatial_grad.shape[1]
    spatial_share = share[0][:spatial_rows].reshape(-1)
    temporal_share = share[0][spatial_rows:].reshape(-1)
    for term in share[1:]:
        spatial_share = spatial_share + term[:spatial_rows].reshape(-1)
        temporal_share = temporal_share + term[spatial_rows:].reshape(-1)
    return (decoded, spatial_share, temporal_share)


def solution(mesh):
    placed = (
        P("dp", None, "space", None, None),
        P("dp"),
        P(),
        P(),
        P(),
        P(),
        P("dp", None),
        P("dp", None, "space", None, None),
    )
    return jax.shard_map(
        on_device,
        mesh=mesh,
        in_specs=placed,
        out_specs=(P("dp", None, "space", None, None), P(("dp", "space")), P(("dp", "space"))),
        check_vma=False,
    )
```

```python
import math

import jax
import jax.numpy as jnp
from jax import lax
from jax.sharding import PartitionSpec as P


def _log2(n):
    b = n.bit_length() - 1
    return b if (1 << b) == n else None


def exchange_rows(cells, axis, dim):
    count = lax.axis_size(axis)
    ends = count - 1
    head = lax.slice_in_dim(cells, 0, 1, axis=dim)
    tail = lax.slice_in_dim(cells, cells.shape[dim] - 1, cells.shape[dim], axis=dim)
    above = lax.ppermute(tail, axis, [(i, i + 1) for i in range(ends)])
    below = lax.ppermute(head, axis, [(i + 1, i) for i in range(ends)])
    return above, below


def upsample(values):
    doubled = jnp.repeat(values, 2, axis=-3)
    return jnp.repeat(doubled, 2, axis=-2)


def silu_slope(pre_act):
    sigmoid_val = jax.nn.sigmoid(pre_act)
    return sigmoid_val * (1.0 + pre_act * (1.0 - sigmoid_val))


def delayed(values, offset):
    if offset == 0:
        return values
    widths = [(0, 0)] * values.ndim
    widths[1] = (offset, 0)
    return jnp.pad(values, widths)[:, : values.shape[1]]


def advanced(values, offset):
    if offset == 0:
        return values
    widths = [(0, 0)] * values.ndim
    widths[1] = (0, offset)
    return jnp.pad(values, widths)[:, offset:]


def space_sum(values):
    count = lax.axis_size("space")
    bits = _log2(count)
    if bits is None:
        return lax.psum(values, "space")
    for bit in range(bits):
        step = 1 << bit
        values = values + lax.ppermute(values, "space", [(i, i ^ step) for i in range(count)])
    return values


def _halve(cur, left, axis, bit, wire=None):
    size = lax.axis_size(axis)
    pos = left.index((axis, bit))
    hi, lo = 1 << pos, 1 << (len(left) - 1 - pos)
    mine = (lax.axis_index(axis) // (1 << bit)) % 2
    v = cur.reshape((hi, 2, lo) + cur.shape[1:])
    keep = lax.dynamic_index_in_dim(v, mine, 1, keepdims=False).reshape((hi * lo,) + cur.shape[1:])
    send = lax.dynamic_index_in_dim(v, 1 - mine, 1, keepdims=False).reshape((hi * lo,) + cur.shape[1:])
    left.remove((axis, bit))
    if wire is not None:
        send = send.astype(wire)
    got = lax.ppermute(send, axis, [(i, i ^ (1 << bit)) for i in range(size)])
    return keep + got.astype(keep.dtype)


def halving_scatter(blocks, orders):
    nd, ns = lax.axis_size("dp"), lax.axis_size("space")
    bd, bs = _log2(nd), _log2(ns)
    if bd is None or bs is None:
        flat = lax.psum_scatter(blocks, "dp", scatter_dimension=0, tiled=True)
        return [lax.psum_scatter(flat, "space", scatter_dimension=0, tiled=True)[0]]
    natural = [("dp", i) for i in reversed(range(bd))] + [("space", i) for i in reversed(range(bs))]
    shared = 0
    while shared < len(natural) and all(o[shared] == orders[0][shared] for o in orders):
        shared += 1
    left = list(natural)
    cur = blocks
    for axis, bit in orders[0][:shared]:
        cur = _halve(cur, left, axis, bit, jnp.bfloat16)
    tail = len(natural)
    while tail > shared and all(o[tail - 1] == orders[0][tail - 1] for o in orders):
        tail -= 1
    width = cur.shape[1] // len(orders)
    outs = []
    for p, order in enumerate(orders):
        part, part_left = cur[:, p * width : (p + 1) * width], list(left)
        for axis, bit in order[shared:tail]:
            part = _halve(part, part_left, axis, bit, jnp.bfloat16)
        outs.append(part)
    cur = jnp.concatenate(outs, axis=1)
    rest = orders[0][tail:]
    if sorted(rest) == [("space", i) for i in range(bs)] and part_left == rest[::-1] == natural[bd:]:
        me = lax.axis_index("space")
        terms = [lax.dynamic_index_in_dim(cur, me, 0, keepdims=False)]
        for shift in range(1, ns):
            send = lax.dynamic_index_in_dim(cur, (me + shift) % ns, 0, keepdims=False)
            got = lax.ppermute(send.astype(jnp.bfloat16), "space", [(i, (i + shift) % ns) for i in range(ns)])
            terms.append(got.astype(cur.dtype))
        return terms
    for axis, bit in rest:
        cur = _halve(cur, part_left, axis, bit)
    return [cur[0]]


def on_device(
    latents,
    lengths,
    spatial_weight,
    temporal_weight,
    critic_weight,
    critic_head,
    critic_frames,
    recon_grad,
):
    groups = lax.axis_size("space")
    devices = lax.axis_size("dp") * groups
    clip_count = latents.shape[0] * lax.axis_size("dp")
    frame_count = latents.shape[1]
    upsampled = upsample(latents)
    above, below = exchange_rows(latents, "space", 2)
    extended = jnp.concatenate(
        [upsample(above)[:, :, 1:], upsampled, upsample(below)[:, :, :1]], axis=2
    )
    padded = jnp.pad(extended, ((0, 0), (0, 0), (0, 0), (1, 1), (0, 0)))
    height = upsampled.shape[2]
    width = upsampled.shape[3]
    pre_act = jnp.zeros(upsampled.shape, jnp.float32)
    for row_tap in range(3):
        for col_tap in range(3):
            window = padded[:, :, row_tap : row_tap + height, col_tap : col_tap + width]
            pre_act = pre_act + jnp.einsum(
                "nfhwc,cd->nfhwd",
                window,
                spatial_weight[row_tap, col_tap],
                preferred_element_type=jnp.float32,
            )
    activated = jax.nn.silu(pre_act).astype(jnp.bfloat16)
    mixing = jnp.zeros(upsampled.shape, jnp.float32)
    for offset in range(3):
        mixing = mixing + jnp.einsum(
            "nfhwc,cd->nfhwd",
            delayed(activated, offset),
            temporal_weight[offset],
            preferred_element_type=jnp.float32,
        )
    alive_mask = (jnp.arange(frame_count)[None, :] < lengths[:, None]).astype(jnp.float32)[
        :, :, None, None, None
    ]
    decoded = (alive_mask * (upsampled.astype(jnp.float32) + mixing)).astype(jnp.bfloat16)
    picker = (critic_frames[:, :, None] == jnp.arange(frame_count)[None, None, :]).astype(
        jnp.bfloat16
    )
    chosen = jnp.einsum(
        "nqf,nfhwc->nqhwc", picker, decoded, preferred_element_type=jnp.float32
    ).astype(jnp.bfloat16)
    hidden = jnp.einsum(
        "nqhwc,ce->nqhwe", chosen, critic_weight, preferred_element_type=jnp.float32
    )
    feature = space_sum(jnp.sum(jax.nn.gelu(hidden), axis=(2, 3))) / (height * groups * width)
    score_val = jnp.sum(feature * critic_head, axis=-1)
    factor = -jax.nn.sigmoid(-score_val)[..., None] * critic_head
    unused, pullback = jax.vjp(jax.nn.gelu, hidden)
    gelu_slope = pullback(jnp.broadcast_to(factor[..., None, None, :], hidden.shape))[0].astype(
        jnp.bfloat16
    )
    slope_rows = jnp.einsum(
        "nqhwe,ce->nqhwc", gelu_slope, critic_weight, preferred_element_type=jnp.float32
    )
    selector = (critic_frames[:, :, None] == jnp.arange(frame_count)[None, None, :]).astype(
        jnp.float32
    )
    adverse_frames = jnp.einsum(
        "nqf,nqhwc->nfhwc", selector, slope_rows, precision=lax.Precision.HIGHEST
    )
    loss_scale = 1.0 / math.sqrt(clip_count * frame_count * height * groups * width)
    cotangent = (
        alive_mask * loss_scale * (recon_grad.astype(jnp.float32) + adverse_frames)
    ).astype(jnp.bfloat16)
    temporal_grad = jnp.stack(
        [
            jnp.einsum(
                "nfhwc,nfhwd->cd",
                delayed(activated, offset),
                cotangent,
                preferred_element_type=jnp.float32,
            )
            for offset in range(3)
        ]
    )
    act_grad = jnp.zeros(upsampled.shape, jnp.float32)
    for offset in range(3):
        act_grad = act_grad + jnp.einsum(
            "nfhwd,cd->nfhwc",
            advanced(cotangent, offset),
            temporal_weight[offset],
            preferred_element_type=jnp.float32,
        )
    pre_slope = (act_grad * silu_slope(pre_act)).astype(jnp.bfloat16)
    tap_grads = []
    for row_tap in range(3):
        for col_tap in range(3):
            window = padded[:, :, row_tap : row_tap + height, col_tap : col_tap + width]
            tap_grads.append(
                jnp.einsum("nfhwc,nfhwd->cd", window, pre_slope, preferred_element_type=jnp.float32)
            )
    channels = spatial_weight.shape[-1]
    spatial_grad = jnp.stack(tap_grads).reshape(devices, -1, channels)
    temporal_grad = temporal_grad.reshape(devices, -1, channels)
    core, x_bit, y_bit = ("dp", 0), ("dp", 1), ("dp", 2)
    z_lo, z_hi = ("space", 0), ("space", 1)
    nd = lax.axis_size("dp")
    if nd == 8 and groups == 4:
        orders = ([core, x_bit, y_bit, z_lo, z_hi], [core, y_bit, x_bit, z_lo, z_hi])
    else:
        plain = [("dp", i) for i in range(nd.bit_length() - 1)]
        orders = (plain + [("space", i) for i in range(groups.bit_length() - 1)],)
    share = halving_scatter(jnp.concatenate([spatial_grad, temporal_grad], axis=1), orders)
    spatial_rows = spatial_grad.shape[1]
    spatial_share = share[0][:spatial_rows].reshape(-1)
    temporal_share = share[0][spatial_rows:].reshape(-1)
    for term in share[1:]:
        spatial_share = spatial_share + term[:spatial_rows].reshape(-1)
        temporal_share = temporal_share + term[spatial_rows:].reshape(-1)
    return (decoded, spatial_share, temporal_share)


def solution(mesh):
    placed = (
        P("dp", None, "space", None, None),
        P("dp"),
        P(),
        P(),
        P(),
        P(),
        P("dp", None),
        P("dp", None, "space", None, None),
    )
    return jax.shard_map(
        on_device,
        mesh=mesh,
        in_specs=placed,
        out_specs=(P("dp", None, "space", None, None), P(("dp", "space")), P(("dp", "space"))),
        check_vma=False,
    )
```

```python
import math

import jax
import jax.numpy as jnp
from jax import lax
from jax.sharding import PartitionSpec as P


def _log2(n):
    b = n.bit_length() - 1
    return b if (1 << b) == n else None


def exchange_rows(cells, axis, dim):
    count = lax.axis_size(axis)
    ends = count - 1
    head = lax.slice_in_dim(cells, 0, 1, axis=dim)
    tail = lax.slice_in_dim(cells, cells.shape[dim] - 1, cells.shape[dim], axis=dim)
    above = lax.ppermute(tail, axis, [(i, i + 1) for i in range(ends)])
    below = lax.ppermute(head, axis, [(i + 1, i) for i in range(ends)])
    return above, below


def upsample(values):
    cols = values.shape[-2]
    spread = (jnp.arange(2 * cols)[:, None] // 2 == jnp.arange(cols)[None, :]).astype(values.dtype)
    wide = jnp.einsum(
        "...wc,vw->...vc", values, spread, preferred_element_type=jnp.float32
    ).astype(values.dtype)
    return jnp.repeat(wide, 2, axis=-3)


def silu_slope(pre_act):
    sigmoid_val = jax.nn.sigmoid(pre_act)
    return sigmoid_val * (1.0 + pre_act * (1.0 - sigmoid_val))


def delayed(values, offset):
    if offset == 0:
        return values
    widths = [(0, 0)] * values.ndim
    widths[1] = (offset, 0)
    return jnp.pad(values, widths)[:, : values.shape[1]]


def advanced(values, offset):
    if offset == 0:
        return values
    widths = [(0, 0)] * values.ndim
    widths[1] = (0, offset)
    return jnp.pad(values, widths)[:, offset:]


def space_sum(values):
    count = lax.axis_size("space")
    bits = _log2(count)
    if bits is None:
        return lax.psum(values, "space")
    for bit in range(bits):
        step = 1 << bit
        values = values + lax.ppermute(values, "space", [(i, i ^ step) for i in range(count)])
    return values


def _halve(cur, left, axis, bit, wire=None):
    size = lax.axis_size(axis)
    pos = left.index((axis, bit))
    hi, lo = 1 << pos, 1 << (len(left) - 1 - pos)
    mine = (lax.axis_index(axis) // (1 << bit)) % 2
    v = cur.reshape((hi, 2, lo) + cur.shape[1:])
    keep = lax.dynamic_index_in_dim(v, mine, 1, keepdims=False).reshape((hi * lo,) + cur.shape[1:])
    send = lax.dynamic_index_in_dim(v, 1 - mine, 1, keepdims=False).reshape((hi * lo,) + cur.shape[1:])
    left.remove((axis, bit))
    if wire is not None:
        send = send.astype(wire)
    got = lax.ppermute(send, axis, [(i, i ^ (1 << bit)) for i in range(size)])
    return keep + got.astype(keep.dtype)


def halving_scatter(blocks, orders):
    nd, ns = lax.axis_size("dp"), lax.axis_size("space")
    bd, bs = _log2(nd), _log2(ns)
    if bd is None or bs is None:
        flat = lax.psum_scatter(blocks, "dp", scatter_dimension=0, tiled=True)
        return [lax.psum_scatter(flat, "space", scatter_dimension=0, tiled=True)[0]]
    natural = [("dp", i) for i in reversed(range(bd))] + [("space", i) for i in reversed(range(bs))]
    shared = 0
    while shared < len(natural) and all(o[shared] == orders[0][shared] for o in orders):
        shared += 1
    left = list(natural)
    cur = blocks
    for axis, bit in orders[0][:shared]:
        cur = _halve(cur, left, axis, bit, jnp.bfloat16)
    tail = len(natural)
    while tail > shared and all(o[tail - 1] == orders[0][tail - 1] for o in orders):
        tail -= 1
    width = cur.shape[1] // len(orders)
    outs = []
    for p, order in enumerate(orders):
        part, part_left = cur[:, p * width : (p + 1) * width], list(left)
        for axis, bit in order[shared:tail]:
            part = _halve(part, part_left, axis, bit, jnp.bfloat16)
        outs.append(part)
    cur = jnp.concatenate(outs, axis=1)
    rest = orders[0][tail:]
    if sorted(rest) == [("space", i) for i in range(bs)] and part_left == rest[::-1] == natural[bd:]:
        me = lax.axis_index("space")
        terms = [lax.dynamic_index_in_dim(cur, me, 0, keepdims=False)]
        for shift in range(1, ns):
            send = lax.dynamic_index_in_dim(cur, (me + shift) % ns, 0, keepdims=False)
            got = lax.ppermute(send.astype(jnp.bfloat16), "space", [(i, (i + shift) % ns) for i in range(ns)])
            terms.append(got.astype(cur.dtype))
        return terms
    for axis, bit in rest:
        cur = _halve(cur, part_left, axis, bit)
    return [cur[0]]


def on_device(
    latents,
    lengths,
    spatial_weight,
    temporal_weight,
    critic_weight,
    critic_head,
    critic_frames,
    recon_grad,
):
    groups = lax.axis_size("space")
    devices = lax.axis_size("dp") * groups
    clip_count = latents.shape[0] * lax.axis_size("dp")
    frame_count = latents.shape[1]
    upsampled = upsample(latents)
    above, below = exchange_rows(latents, "space", 2)
    extended = jnp.concatenate(
        [upsample(above)[:, :, 1:], upsampled, upsample(below)[:, :, :1]], axis=2
    )
    padded = jnp.pad(extended, ((0, 0), (0, 0), (0, 0), (1, 1), (0, 0)))
    height = upsampled.shape[2]
    width = upsampled.shape[3]
    pre_act = jnp.zeros(upsampled.shape, jnp.float32)
    for row_tap in range(3):
        for col_tap in range(3):
            window = padded[:, :, row_tap : row_tap + height, col_tap : col_tap + width]
            pre_act = pre_act + jnp.einsum(
                "nfhwc,cd->nfhwd",
                window,
                spatial_weight[row_tap, col_tap],
                preferred_element_type=jnp.float32,
            )
    activated = jax.nn.silu(pre_act).astype(jnp.bfloat16)
    mixing = jnp.zeros(upsampled.shape, jnp.float32)
    for offset in range(3):
        mixing = mixing + jnp.einsum(
            "nfhwc,cd->nfhwd",
            delayed(activated, offset),
            temporal_weight[offset],
            preferred_element_type=jnp.float32,
        )
    alive_mask = (jnp.arange(frame_count)[None, :] < lengths[:, None]).astype(jnp.float32)[
        :, :, None, None, None
    ]
    decoded = (alive_mask * (upsampled.astype(jnp.float32) + mixing)).astype(jnp.bfloat16)
    picker = (critic_frames[:, :, None] == jnp.arange(frame_count)[None, None, :]).astype(
        jnp.bfloat16
    )
    chosen = jnp.einsum(
        "nqf,nfhwc->nqhwc", picker, decoded, preferred_element_type=jnp.float32
    ).astype(jnp.bfloat16)
    hidden = jnp.einsum(
        "nqhwc,ce->nqhwe", chosen, critic_weight, preferred_element_type=jnp.float32
    )
    feature = space_sum(jnp.sum(jax.nn.gelu(hidden), axis=(2, 3))) / (height * groups * width)
    score_val = jnp.sum(feature * critic_head, axis=-1)
    factor = -jax.nn.sigmoid(-score_val)[..., None] * critic_head
    unused, pullback = jax.vjp(jax.nn.gelu, hidden)
    gelu_slope = pullback(jnp.broadcast_to(factor[..., None, None, :], hidden.shape))[0].astype(
        jnp.bfloat16
    )
    slope_rows = jnp.einsum(
        "nqhwe,ce->nqhwc", gelu_slope, critic_weight, preferred_element_type=jnp.float32
    )
    selector = (critic_frames[:, :, None] == jnp.arange(frame_count)[None, None, :]).astype(
        jnp.float32
    )
    adverse_frames = jnp.einsum(
        "nqf,nqhwc->nfhwc", selector, slope_rows, precision=lax.Precision.HIGHEST
    )
    loss_scale = 1.0 / math.sqrt(clip_count * frame_count * height * groups * width)
    cotangent = (
        alive_mask * loss_scale * (recon_grad.astype(jnp.float32) + adverse_frames)
    ).astype(jnp.bfloat16)
    temporal_grad = jnp.stack(
        [
            jnp.einsum(
                "nfhwc,nfhwd->cd",
                delayed(activated, offset),
                cotangent,
                preferred_element_type=jnp.float32,
            )
            for offset in range(3)
        ]
    )
    act_grad = jnp.zeros(upsampled.shape, jnp.float32)
    for offset in range(3):
        act_grad = act_grad + jnp.einsum(
            "nfhwd,cd->nfhwc",
            advanced(cotangent, offset),
            temporal_weight[offset],
            preferred_element_type=jnp.float32,
        )
    pre_slope = (act_grad * silu_slope(pre_act)).astype(jnp.bfloat16)
    tap_grads = []
    for row_tap in range(3):
        for col_tap in range(3):
            window = padded[:, :, row_tap : row_tap + height, col_tap : col_tap + width]
            tap_grads.append(
                jnp.einsum("nfhwc,nfhwd->cd", window, pre_slope, preferred_element_type=jnp.float32)
            )
    channels = spatial_weight.shape[-1]
    spatial_grad = jnp.stack(tap_grads).reshape(devices, -1, channels)
    temporal_grad = temporal_grad.reshape(devices, -1, channels)
    core, x_bit, y_bit = ("dp", 0), ("dp", 1), ("dp", 2)
    z_lo, z_hi = ("space", 0), ("space", 1)
    nd = lax.axis_size("dp")
    if nd == 8 and groups == 4:
        orders = ([core, x_bit, y_bit, z_lo, z_hi], [core, y_bit, x_bit, z_lo, z_hi])
    else:
        plain = [("dp", i) for i in range(nd.bit_length() - 1)]
        orders = (plain + [("space", i) for i in range(groups.bit_length() - 1)],)
    share = halving_scatter(jnp.concatenate([spatial_grad, temporal_grad], axis=1), orders)
    spatial_rows = spatial_grad.shape[1]
    spatial_share = share[0][:spatial_rows].reshape(-1)
    temporal_share = share[0][spatial_rows:].reshape(-1)
    for term in share[1:]:
        spatial_share = spatial_share + term[:spatial_rows].reshape(-1)
        temporal_share = temporal_share + term[spatial_rows:].reshape(-1)
    return (decoded, spatial_share, temporal_share)


def solution(mesh):
    placed = (
        P("dp", None, "space", None, None),
        P("dp"),
        P(),
        P(),
        P(),
        P(),
        P("dp", None),
        P("dp", None, "space", None, None),
    )
    return jax.shard_map(
        on_device,
        mesh=mesh,
        in_specs=placed,
        out_specs=(P("dp", None, "space", None, None), P(("dp", "space")), P(("dp", "space"))),
        check_vma=False,
    )
```

```python
import math

import jax
import jax.numpy as jnp
from jax import lax
from jax.sharding import PartitionSpec as P


def _log2(n):
    b = n.bit_length() - 1
    return b if (1 << b) == n else None


def exchange_rows(cells, axis, dim):
    count = lax.axis_size(axis)
    ends = count - 1
    head = lax.slice_in_dim(cells, 0, 1, axis=dim)
    tail = lax.slice_in_dim(cells, cells.shape[dim] - 1, cells.shape[dim], axis=dim)
    above = lax.ppermute(tail, axis, [(i, i + 1) for i in range(ends)])
    below = lax.ppermute(head, axis, [(i + 1, i) for i in range(ends)])
    return above, below


def upsample(values):
    doubled = jnp.repeat(values, 2, axis=-3)
    return jnp.repeat(doubled, 2, axis=-2)


def silu_slope(pre_act):
    sigmoid_val = jax.nn.sigmoid(pre_act)
    return sigmoid_val * (1.0 + pre_act * (1.0 - sigmoid_val))


def delayed(values, offset):
    if offset == 0:
        return values
    widths = [(0, 0)] * values.ndim
    widths[1] = (offset, 0)
    return jnp.pad(values, widths)[:, : values.shape[1]]


def advanced(values, offset):
    if offset == 0:
        return values
    widths = [(0, 0)] * values.ndim
    widths[1] = (0, offset)
    return jnp.pad(values, widths)[:, offset:]


def space_sum(values):
    count = lax.axis_size("space")
    bits = _log2(count)
    if bits is None:
        return lax.psum(values, "space")
    for bit in range(bits):
        step = 1 << bit
        values = values + lax.ppermute(values, "space", [(i, i ^ step) for i in range(count)])
    return values


def _halve(cur, left, axis, bit, wire=None):
    size = lax.axis_size(axis)
    pos = left.index((axis, bit))
    hi, lo = 1 << pos, 1 << (len(left) - 1 - pos)
    mine = (lax.axis_index(axis) // (1 << bit)) % 2
    v = cur.reshape((hi, 2, lo) + cur.shape[1:])
    keep = lax.dynamic_index_in_dim(v, mine, 1, keepdims=False).reshape((hi * lo,) + cur.shape[1:])
    send = lax.dynamic_index_in_dim(v, 1 - mine, 1, keepdims=False).reshape((hi * lo,) + cur.shape[1:])
    left.remove((axis, bit))
    if wire is not None:
        send = send.astype(wire)
    got = lax.ppermute(send, axis, [(i, i ^ (1 << bit)) for i in range(size)])
    return keep + got.astype(keep.dtype)


def halving_scatter(blocks, orders):
    nd, ns = lax.axis_size("dp"), lax.axis_size("space")
    bd, bs = _log2(nd), _log2(ns)
    if bd is None or bs is None:
        flat = lax.psum_scatter(blocks, "dp", scatter_dimension=0, tiled=True)
        return [lax.psum_scatter(flat, "space", scatter_dimension=0, tiled=True)[0]]
    natural = [("dp", i) for i in reversed(range(bd))] + [("space", i) for i in reversed(range(bs))]
    shared = 0
    while shared < len(natural) and all(o[shared] == orders[0][shared] for o in orders):
        shared += 1
    left = list(natural)
    cur = blocks
    for axis, bit in orders[0][:shared]:
        cur = _halve(cur, left, axis, bit, jnp.bfloat16)
    tail = len(natural)
    while tail > shared and all(o[tail - 1] == orders[0][tail - 1] for o in orders):
        tail -= 1
    width = cur.shape[1] // len(orders)
    outs = []
    for p, order in enumerate(orders):
        part, part_left = cur[:, p * width : (p + 1) * width], list(left)
        for axis, bit in order[shared:tail]:
            part = _halve(part, part_left, axis, bit, jnp.bfloat16)
        outs.append(part)
    cur = jnp.concatenate(outs, axis=1)
    rest = orders[0][tail:]
    if sorted(rest) == [("space", i) for i in range(bs)] and part_left == rest[::-1] == natural[bd:]:
        me = lax.axis_index("space")
        terms = [lax.dynamic_index_in_dim(cur, me, 0, keepdims=False)]
        for shift in range(1, ns):
            send = lax.dynamic_index_in_dim(cur, (me + shift) % ns, 0, keepdims=False)
            got = lax.ppermute(send.astype(jnp.bfloat16), "space", [(i, (i + shift) % ns) for i in range(ns)])
            terms.append(got.astype(cur.dtype))
        return terms
    for axis, bit in rest:
        cur = _halve(cur, part_left, axis, bit)
    return [cur[0]]


def on_device(
    latents,
    lengths,
    spatial_weight,
    temporal_weight,
    critic_weight,
    critic_head,
    critic_frames,
    recon_grad,
):
    groups = lax.axis_size("space")
    devices = lax.axis_size("dp") * groups
    clip_count = latents.shape[0] * lax.axis_size("dp")
    frame_count = latents.shape[1]
    upsampled = upsample(latents)
    above, below = exchange_rows(latents, "space", 2)
    extended = jnp.concatenate(
        [upsample(above)[:, :, 1:], upsampled, upsample(below)[:, :, :1]], axis=2
    )
    padded = jnp.pad(extended, ((0, 0), (0, 0), (0, 0), (1, 1), (0, 0)))
    height = upsampled.shape[2]
    width = upsampled.shape[3]
    pre_act = jnp.zeros(upsampled.shape, jnp.float32)
    for row_tap in range(3):
        for col_tap in range(3):
            window = padded[:, :, row_tap : row_tap + height, col_tap : col_tap + width]
            pre_act = pre_act + jnp.einsum(
                "nfhwc,cd->nfhwd",
                window,
                spatial_weight[row_tap, col_tap],
                preferred_element_type=jnp.float32,
            )
    activated = jax.nn.silu(pre_act).astype(jnp.bfloat16)
    mixing = jnp.zeros(upsampled.shape, jnp.float32)
    for offset in range(3):
        mixing = mixing + jnp.einsum(
            "nfhwc,cd->nfhwd",
            delayed(activated, offset),
            temporal_weight[offset],
            preferred_element_type=jnp.float32,
        )
    alive_mask = (jnp.arange(frame_count)[None, :] < lengths[:, None]).astype(jnp.float32)[
        :, :, None, None, None
    ]
    decoded = (alive_mask * (upsampled.astype(jnp.float32) + mixing)).astype(jnp.bfloat16)
    picker = (critic_frames[:, :, None] == jnp.arange(frame_count)[None, None, :]).astype(
        jnp.bfloat16
    )
    chosen = jnp.einsum(
        "nqf,nfhwc->nqhwc", picker, decoded, preferred_element_type=jnp.float32
    ).astype(jnp.bfloat16)
    hidden = jnp.einsum(
        "nqhwc,ce->nqhwe", chosen, critic_weight, preferred_element_type=jnp.float32
    )
    feature = space_sum(jnp.sum(jax.nn.gelu(hidden), axis=(2, 3))) / (height * groups * width)
    score_val = jnp.sum(feature * critic_head, axis=-1)
    factor = -jax.nn.sigmoid(-score_val)[..., None] * critic_head
    unused, pullback = jax.vjp(jax.nn.gelu, hidden)
    gelu_slope = pullback(jnp.broadcast_to(factor[..., None, None, :], hidden.shape))[0].astype(
        jnp.bfloat16
    )
    slope_rows = jnp.einsum(
        "nqhwe,ce->nqhwc", gelu_slope, critic_weight, preferred_element_type=jnp.float32
    )
    selector = (critic_frames[:, :, None] == jnp.arange(frame_count)[None, None, :]).astype(
        jnp.float32
    )
    adverse_frames = jnp.einsum(
        "nqf,nqhwc->nfhwc", selector, slope_rows, precision=lax.Precision.HIGHEST
    )
    loss_scale = 1.0 / math.sqrt(clip_count * frame_count * height * groups * width)
    cotangent = (
        alive_mask * loss_scale * (recon_grad.astype(jnp.float32) + adverse_frames)
    ).astype(jnp.bfloat16)
    temporal_grad = jnp.stack(
        [
            jnp.einsum(
                "nfhwc,nfhwd->cd",
                delayed(activated, offset),
                cotangent,
                preferred_element_type=jnp.float32,
            )
            for offset in range(3)
        ]
    )
    act_grad = jnp.zeros(upsampled.shape, jnp.float32)
    for offset in range(3):
        act_grad = act_grad + jnp.einsum(
            "nfhwd,cd->nfhwc",
            advanced(cotangent, offset),
            temporal_weight[offset],
            preferred_element_type=jnp.float32,
        )
    pre_slope = (act_grad * silu_slope(pre_act)).astype(jnp.bfloat16)
    windows = jnp.stack(
        [
            padded[:, :, row_tap : row_tap + height, col_tap : col_tap + width]
            for row_tap in range(3)
            for col_tap in range(3)
        ]
    )
    spatial_grad = jnp.einsum(
        "tnfhwc,nfhwd->tcd", windows, pre_slope, preferred_element_type=jnp.float32
    )
    channels = spatial_weight.shape[-1]
    spatial_grad = spatial_grad.reshape(devices, -1, channels)
    temporal_grad = temporal_grad.reshape(devices, -1, channels)
    core, x_bit, y_bit = ("dp", 0), ("dp", 1), ("dp", 2)
    z_lo, z_hi = ("space", 0), ("space", 1)
    nd = lax.axis_size("dp")
    if nd == 8 and groups == 4:
        orders = ([core, x_bit, y_bit, z_lo, z_hi], [core, y_bit, x_bit, z_lo, z_hi])
    else:
        plain = [("dp", i) for i in range(nd.bit_length() - 1)]
        orders = (plain + [("space", i) for i in range(groups.bit_length() - 1)],)
    share = halving_scatter(jnp.concatenate([spatial_grad, temporal_grad], axis=1), orders)
    spatial_rows = spatial_grad.shape[1]
    spatial_share = share[0][:spatial_rows].reshape(-1)
    temporal_share = share[0][spatial_rows:].reshape(-1)
    for term in share[1:]:
        spatial_share = spatial_share + term[:spatial_rows].reshape(-1)
        temporal_share = temporal_share + term[spatial_rows:].reshape(-1)
    return (decoded, spatial_share, temporal_share)


def solution(mesh):
    placed = (
        P("dp", None, "space", None, None),
        P("dp"),
        P(),
        P(),
        P(),
        P(),
        P("dp", None),
        P("dp", None, "space", None, None),
    )
    return jax.shard_map(
        on_device,
        mesh=mesh,
        in_specs=placed,
        out_specs=(P("dp", None, "space", None, None), P(("dp", "space")), P(("dp", "space"))),
        check_vma=False,
    )
```

```python
import math

import jax
import jax.numpy as jnp
from jax import lax
from jax.sharding import PartitionSpec as P


def _log2(n):
    b = n.bit_length() - 1
    return b if (1 << b) == n else None


def exchange_rows(cells, axis, dim):
    count = lax.axis_size(axis)
    ends = count - 1
    head = lax.slice_in_dim(cells, 0, 1, axis=dim)
    tail = lax.slice_in_dim(cells, cells.shape[dim] - 1, cells.shape[dim], axis=dim)
    above = lax.ppermute(tail, axis, [(i, i + 1) for i in range(ends)])
    below = lax.ppermute(head, axis, [(i + 1, i) for i in range(ends)])
    return above, below


def upsample(values):
    doubled = jnp.repeat(values, 2, axis=-3)
    return jnp.repeat(doubled, 2, axis=-2)


def silu_slope(pre_act):
    sigmoid_val = jax.nn.sigmoid(pre_act)
    return sigmoid_val * (1.0 + pre_act * (1.0 - sigmoid_val))


def delayed(values, offset):
    if offset == 0:
        return values
    widths = [(0, 0)] * values.ndim
    widths[1] = (offset, 0)
    return jnp.pad(values, widths)[:, : values.shape[1]]


def advanced(values, offset):
    if offset == 0:
        return values
    widths = [(0, 0)] * values.ndim
    widths[1] = (0, offset)
    return jnp.pad(values, widths)[:, offset:]


def space_sum(values):
    count = lax.axis_size("space")
    bits = _log2(count)
    if bits is None:
        return lax.psum(values, "space")
    for bit in range(bits):
        step = 1 << bit
        values = values + lax.ppermute(values, "space", [(i, i ^ step) for i in range(count)])
    return values


def _halve(cur, left, axis, bit, wire=None):
    size = lax.axis_size(axis)
    pos = left.index((axis, bit))
    hi, lo = 1 << pos, 1 << (len(left) - 1 - pos)
    mine = (lax.axis_index(axis) // (1 << bit)) % 2
    v = cur.reshape((hi, 2, lo) + cur.shape[1:])
    keep = lax.dynamic_index_in_dim(v, mine, 1, keepdims=False).reshape((hi * lo,) + cur.shape[1:])
    send = lax.dynamic_index_in_dim(v, 1 - mine, 1, keepdims=False).reshape((hi * lo,) + cur.shape[1:])
    left.remove((axis, bit))
    if wire is not None:
        send = send.astype(wire)
    got = lax.ppermute(send, axis, [(i, i ^ (1 << bit)) for i in range(size)])
    return keep + got.astype(keep.dtype)


def halving_scatter(blocks, orders):
    nd, ns = lax.axis_size("dp"), lax.axis_size("space")
    bd, bs = _log2(nd), _log2(ns)
    if bd is None or bs is None:
        flat = lax.psum_scatter(blocks, "dp", scatter_dimension=0, tiled=True)
        return [lax.psum_scatter(flat, "space", scatter_dimension=0, tiled=True)[0]]
    natural = [("dp", i) for i in reversed(range(bd))] + [("space", i) for i in reversed(range(bs))]
    shared = 0
    while shared < len(natural) and all(o[shared] == orders[0][shared] for o in orders):
        shared += 1
    left = list(natural)
    cur = blocks
    for axis, bit in orders[0][:shared]:
        cur = _halve(cur, left, axis, bit, jnp.bfloat16)
    tail = len(natural)
    while tail > shared and all(o[tail - 1] == orders[0][tail - 1] for o in orders):
        tail -= 1
    rows = cur.shape[1]
    if len(orders) == 2 and rows % 16 == 0:
        cuts = [0, rows // 2 + 8, rows]
    else:
        cuts = [p * rows // len(orders) for p in range(len(orders) + 1)]
    outs = []
    for p, order in enumerate(orders):
        part, part_left = cur[:, cuts[p] : cuts[p + 1]], list(left)
        for axis, bit in order[shared:tail]:
            part = _halve(part, part_left, axis, bit, jnp.bfloat16)
        outs.append(part)
    cur = jnp.concatenate(outs, axis=1)
    rest = orders[0][tail:]
    if sorted(rest) == [("space", i) for i in range(bs)] and part_left == rest[::-1] == natural[bd:]:
        me = lax.axis_index("space")
        terms = [lax.dynamic_index_in_dim(cur, me, 0, keepdims=False)]
        for shift in range(1, ns):
            send = lax.dynamic_index_in_dim(cur, (me + shift) % ns, 0, keepdims=False)
            got = lax.ppermute(send.astype(jnp.bfloat16), "space", [(i, (i + shift) % ns) for i in range(ns)])
            terms.append(got.astype(cur.dtype))
        return terms
    for axis, bit in rest:
        cur = _halve(cur, part_left, axis, bit)
    return [cur[0]]


def on_device(
    latents,
    lengths,
    spatial_weight,
    temporal_weight,
    critic_weight,
    critic_head,
    critic_frames,
    recon_grad,
):
    groups = lax.axis_size("space")
    devices = lax.axis_size("dp") * groups
    clip_count = latents.shape[0] * lax.axis_size("dp")
    frame_count = latents.shape[1]
    upsampled = upsample(latents)
    above, below = exchange_rows(latents, "space", 2)
    extended = jnp.concatenate(
        [upsample(above)[:, :, 1:], upsampled, upsample(below)[:, :, :1]], axis=2
    )
    padded = jnp.pad(extended, ((0, 0), (0, 0), (0, 0), (1, 1), (0, 0)))
    height = upsampled.shape[2]
    width = upsampled.shape[3]
    pre_act = jnp.zeros(upsampled.shape, jnp.float32)
    for row_tap in range(3):
        for col_tap in range(3):
            window = padded[:, :, row_tap : row_tap + height, col_tap : col_tap + width]
            pre_act = pre_act + jnp.einsum(
                "nfhwc,cd->nfhwd",
                window,
                spatial_weight[row_tap, col_tap],
                preferred_element_type=jnp.float32,
            )
    activated = jax.nn.silu(pre_act).astype(jnp.bfloat16)
    mixing = jnp.zeros(upsampled.shape, jnp.float32)
    for offset in range(3):
        mixing = mixing + jnp.einsum(
            "nfhwc,cd->nfhwd",
            delayed(activated, offset),
            temporal_weight[offset],
            preferred_element_type=jnp.float32,
        )
    alive_mask = (jnp.arange(frame_count)[None, :] < lengths[:, None]).astype(jnp.float32)[
        :, :, None, None, None
    ]
    decoded = (alive_mask * (upsampled.astype(jnp.float32) + mixing)).astype(jnp.bfloat16)
    picker = (critic_frames[:, :, None] == jnp.arange(frame_count)[None, None, :]).astype(
        jnp.bfloat16
    )
    chosen = jnp.einsum(
        "nqf,nfhwc->nqhwc", picker, decoded, preferred_element_type=jnp.float32
    ).astype(jnp.bfloat16)
    hidden = jnp.einsum(
        "nqhwc,ce->nqhwe", chosen, critic_weight, preferred_element_type=jnp.float32
    )
    feature = space_sum(jnp.sum(jax.nn.gelu(hidden), axis=(2, 3))) / (height * groups * width)
    score_val = jnp.sum(feature * critic_head, axis=-1)
    factor = -jax.nn.sigmoid(-score_val)[..., None] * critic_head
    unused, pullback = jax.vjp(jax.nn.gelu, hidden)
    gelu_slope = pullback(jnp.broadcast_to(factor[..., None, None, :], hidden.shape))[0].astype(
        jnp.bfloat16
    )
    slope_rows = jnp.einsum(
        "nqhwe,ce->nqhwc", gelu_slope, critic_weight, preferred_element_type=jnp.float32
    )
    selector = (critic_frames[:, :, None] == jnp.arange(frame_count)[None, None, :]).astype(
        jnp.float32
    )
    adverse_frames = jnp.einsum(
        "nqf,nqhwc->nfhwc", selector, slope_rows, precision=lax.Precision.HIGHEST
    )
    loss_scale = 1.0 / math.sqrt(clip_count * frame_count * height * groups * width)
    cotangent = (
        alive_mask * loss_scale * (recon_grad.astype(jnp.float32) + adverse_frames)
    ).astype(jnp.bfloat16)
    temporal_grad = jnp.stack(
        [
            jnp.einsum(
                "nfhwc,nfhwd->cd",
                delayed(activated, offset),
                cotangent,
                preferred_element_type=jnp.float32,
            )
            for offset in range(3)
        ]
    )
    act_grad = jnp.zeros(upsampled.shape, jnp.float32)
    for offset in range(3):
        act_grad = act_grad + jnp.einsum(
            "nfhwd,cd->nfhwc",
            advanced(cotangent, offset),
            temporal_weight[offset],
            preferred_element_type=jnp.float32,
        )
    pre_slope = (act_grad * silu_slope(pre_act)).astype(jnp.bfloat16)
    tap_grads = []
    for row_tap in range(3):
        for col_tap in range(3):
            window = padded[:, :, row_tap : row_tap + height, col_tap : col_tap + width]
            tap_grads.append(
                jnp.einsum("nfhwc,nfhwd->cd", window, pre_slope, preferred_element_type=jnp.float32)
            )
    channels = spatial_weight.shape[-1]
    spatial_grad = jnp.stack(tap_grads).reshape(devices, -1, channels)
    temporal_grad = temporal_grad.reshape(devices, -1, channels)
    core, x_bit, y_bit = ("dp", 0), ("dp", 1), ("dp", 2)
    z_lo, z_hi = ("space", 0), ("space", 1)
    nd = lax.axis_size("dp")
    if nd == 8 and groups == 4:
        orders = ([core, x_bit, y_bit, z_lo, z_hi], [core, y_bit, x_bit, z_lo, z_hi])
    else:
        plain = [("dp", i) for i in range(nd.bit_length() - 1)]
        orders = (plain + [("space", i) for i in range(groups.bit_length() - 1)],)
    share = halving_scatter(jnp.concatenate([spatial_grad, temporal_grad], axis=1), orders)
    spatial_rows = spatial_grad.shape[1]
    spatial_share = share[0][:spatial_rows].reshape(-1)
    temporal_share = share[0][spatial_rows:].reshape(-1)
    for term in share[1:]:
        spatial_share = spatial_share + term[:spatial_rows].reshape(-1)
        temporal_share = temporal_share + term[spatial_rows:].reshape(-1)
    return (decoded, spatial_share, temporal_share)


def solution(mesh):
    placed = (
        P("dp", None, "space", None, None),
        P("dp"),
        P(),
        P(),
        P(),
        P(),
        P("dp", None),
        P("dp", None, "space", None, None),
    )
    return jax.shard_map(
        on_device,
        mesh=mesh,
        in_specs=placed,
        out_specs=(P("dp", None, "space", None, None), P(("dp", "space")), P(("dp", "space"))),
        check_vma=False,
    )
```

```python
import math

import jax
import jax.numpy as jnp
from jax import lax
from jax.sharding import PartitionSpec as P


def _log2(n):
    b = n.bit_length() - 1
    return b if (1 << b) == n else None


def exchange_rows(cells, axis, dim):
    count = lax.axis_size(axis)
    ends = count - 1
    head = lax.slice_in_dim(cells, 0, 1, axis=dim)
    tail = lax.slice_in_dim(cells, cells.shape[dim] - 1, cells.shape[dim], axis=dim)
    above = lax.ppermute(tail, axis, [(i, i + 1) for i in range(ends)])
    below = lax.ppermute(head, axis, [(i + 1, i) for i in range(ends)])
    return above, below


def upsample(values):
    doubled = jnp.repeat(values, 2, axis=-3)
    return jnp.repeat(doubled, 2, axis=-2)


def silu_slope(pre_act):
    sigmoid_val = jax.nn.sigmoid(pre_act)
    return sigmoid_val * (1.0 + pre_act * (1.0 - sigmoid_val))


def delayed(values, offset):
    if offset == 0:
        return values
    widths = [(0, 0)] * values.ndim
    widths[1] = (offset, 0)
    return jnp.pad(values, widths)[:, : values.shape[1]]


def advanced(values, offset):
    if offset == 0:
        return values
    widths = [(0, 0)] * values.ndim
    widths[1] = (0, offset)
    return jnp.pad(values, widths)[:, offset:]


def space_sum(values):
    count = lax.axis_size("space")
    bits = _log2(count)
    if bits is None:
        return lax.psum(values, "space")
    for bit in range(bits):
        step = 1 << bit
        values = values + lax.ppermute(values, "space", [(i, i ^ step) for i in range(count)])
    return values


def _halve(cur, left, axis, bit, wire=None):
    size = lax.axis_size(axis)
    pos = left.index((axis, bit))
    hi, lo = 1 << pos, 1 << (len(left) - 1 - pos)
    mine = (lax.axis_index(axis) // (1 << bit)) % 2
    v = cur.reshape((hi, 2, lo) + cur.shape[1:])
    keep = lax.dynamic_index_in_dim(v, mine, 1, keepdims=False).reshape((hi * lo,) + cur.shape[1:])
    send = lax.dynamic_index_in_dim(v, 1 - mine, 1, keepdims=False).reshape((hi * lo,) + cur.shape[1:])
    left.remove((axis, bit))
    if wire is not None:
        send = send.astype(wire)
    got = lax.ppermute(send, axis, [(i, i ^ (1 << bit)) for i in range(size)])
    return keep + got.astype(keep.dtype)


def halving_scatter(blocks, orders):
    nd, ns = lax.axis_size("dp"), lax.axis_size("space")
    bd, bs = _log2(nd), _log2(ns)
    if bd is None or bs is None:
        flat = lax.psum_scatter(blocks, "dp", scatter_dimension=0, tiled=True)
        return [lax.psum_scatter(flat, "space", scatter_dimension=0, tiled=True)[0]]
    natural = [("dp", i) for i in reversed(range(bd))] + [("space", i) for i in reversed(range(bs))]
    shared = 0
    while shared < len(natural) and all(o[shared] == orders[0][shared] for o in orders):
        shared += 1
    left = list(natural)
    cur = blocks
    for axis, bit in orders[0][:shared]:
        cur = _halve(cur, left, axis, bit, jnp.bfloat16)
    tail = len(natural)
    while tail > shared and all(o[tail - 1] == orders[0][tail - 1] for o in orders):
        tail -= 1
    rows = cur.shape[1]
    if len(orders) == 2 and rows % 16 == 0:
        cuts = [0, rows // 2 - 8, rows]
    else:
        cuts = [p * rows // len(orders) for p in range(len(orders) + 1)]
    outs = []
    for p, order in enumerate(orders):
        part, part_left = cur[:, cuts[p] : cuts[p + 1]], list(left)
        for axis, bit in order[shared:tail]:
            part = _halve(part, part_left, axis, bit, jnp.bfloat16)
        outs.append(part)
    cur = jnp.concatenate(outs, axis=1)
    rest = orders[0][tail:]
    if sorted(rest) == [("space", i) for i in range(bs)] and part_left == rest[::-1] == natural[bd:]:
        me = lax.axis_index("space")
        terms = [lax.dynamic_index_in_dim(cur, me, 0, keepdims=False)]
        for shift in range(1, ns):
            send = lax.dynamic_index_in_dim(cur, (me + shift) % ns, 0, keepdims=False)
            got = lax.ppermute(send.astype(jnp.bfloat16), "space", [(i, (i + shift) % ns) for i in range(ns)])
            terms.append(got.astype(cur.dtype))
        return terms
    for axis, bit in rest:
        cur = _halve(cur, part_left, axis, bit)
    return [cur[0]]


def on_device(
    latents,
    lengths,
    spatial_weight,
    temporal_weight,
    critic_weight,
    critic_head,
    critic_frames,
    recon_grad,
):
    groups = lax.axis_size("space")
    devices = lax.axis_size("dp") * groups
    clip_count = latents.shape[0] * lax.axis_size("dp")
    frame_count = latents.shape[1]
    upsampled = upsample(latents)
    above, below = exchange_rows(latents, "space", 2)
    extended = jnp.concatenate(
        [upsample(above)[:, :, 1:], upsampled, upsample(below)[:, :, :1]], axis=2
    )
    padded = jnp.pad(extended, ((0, 0), (0, 0), (0, 0), (1, 1), (0, 0)))
    height = upsampled.shape[2]
    width = upsampled.shape[3]
    pre_act = jnp.zeros(upsampled.shape, jnp.float32)
    for row_tap in range(3):
        for col_tap in range(3):
            window = padded[:, :, row_tap : row_tap + height, col_tap : col_tap + width]
            pre_act = pre_act + jnp.einsum(
                "nfhwc,cd->nfhwd",
                window,
                spatial_weight[row_tap, col_tap],
                preferred_element_type=jnp.float32,
            )
    activated = jax.nn.silu(pre_act).astype(jnp.bfloat16)
    mixing = jnp.zeros(upsampled.shape, jnp.float32)
    for offset in range(3):
        mixing = mixing + jnp.einsum(
            "nfhwc,cd->nfhwd",
            delayed(activated, offset),
            temporal_weight[offset],
            preferred_element_type=jnp.float32,
        )
    alive_mask = (jnp.arange(frame_count)[None, :] < lengths[:, None]).astype(jnp.float32)[
        :, :, None, None, None
    ]
    decoded = (alive_mask * (upsampled.astype(jnp.float32) + mixing)).astype(jnp.bfloat16)
    picker = (critic_frames[:, :, None] == jnp.arange(frame_count)[None, None, :]).astype(
        jnp.bfloat16
    )
    chosen = jnp.einsum(
        "nqf,nfhwc->nqhwc", picker, decoded, preferred_element_type=jnp.float32
    ).astype(jnp.bfloat16)
    hidden = jnp.einsum(
        "nqhwc,ce->nqhwe", chosen, critic_weight, preferred_element_type=jnp.float32
    )
    feature = space_sum(jnp.sum(jax.nn.gelu(hidden), axis=(2, 3))) / (height * groups * width)
    score_val = jnp.sum(feature * critic_head, axis=-1)
    factor = -jax.nn.sigmoid(-score_val)[..., None] * critic_head
    unused, pullback = jax.vjp(jax.nn.gelu, hidden)
    gelu_slope = pullback(jnp.broadcast_to(factor[..., None, None, :], hidden.shape))[0].astype(
        jnp.bfloat16
    )
    slope_rows = jnp.einsum(
        "nqhwe,ce->nqhwc", gelu_slope, critic_weight, preferred_element_type=jnp.float32
    )
    selector = (critic_frames[:, :, None] == jnp.arange(frame_count)[None, None, :]).astype(
        jnp.float32
    )
    adverse_frames = jnp.einsum(
        "nqf,nqhwc->nfhwc", selector, slope_rows, precision=lax.Precision.HIGHEST
    )
    loss_scale = 1.0 / math.sqrt(clip_count * frame_count * height * groups * width)
    cotangent = (
        alive_mask * loss_scale * (recon_grad.astype(jnp.float32) + adverse_frames)
    ).astype(jnp.bfloat16)
    temporal_grad = jnp.stack(
        [
            jnp.einsum(
                "nfhwc,nfhwd->cd",
                delayed(activated, offset),
                cotangent,
                preferred_element_type=jnp.float32,
            )
            for offset in range(3)
        ]
    )
    act_grad = jnp.zeros(upsampled.shape, jnp.float32)
    for offset in range(3):
        act_grad = act_grad + jnp.einsum(
            "nfhwd,cd->nfhwc",
            advanced(cotangent, offset),
            temporal_weight[offset],
            preferred_element_type=jnp.float32,
        )
    pre_slope = (act_grad * silu_slope(pre_act)).astype(jnp.bfloat16)
    tap_grads = []
    for row_tap in range(3):
        for col_tap in range(3):
            window = padded[:, :, row_tap : row_tap + height, col_tap : col_tap + width]
            tap_grads.append(
                jnp.einsum("nfhwc,nfhwd->cd", window, pre_slope, preferred_element_type=jnp.float32)
            )
    channels = spatial_weight.shape[-1]
    spatial_grad = jnp.stack(tap_grads).reshape(devices, -1, channels)
    temporal_grad = temporal_grad.reshape(devices, -1, channels)
    core, x_bit, y_bit = ("dp", 0), ("dp", 1), ("dp", 2)
    z_lo, z_hi = ("space", 0), ("space", 1)
    nd = lax.axis_size("dp")
    if nd == 8 and groups == 4:
        orders = ([core, x_bit, y_bit, z_lo, z_hi], [core, y_bit, x_bit, z_lo, z_hi])
    else:
        plain = [("dp", i) for i in range(nd.bit_length() - 1)]
        orders = (plain + [("space", i) for i in range(groups.bit_length() - 1)],)
    share = halving_scatter(jnp.concatenate([spatial_grad, temporal_grad], axis=1), orders)
    spatial_rows = spatial_grad.shape[1]
    spatial_share = share[0][:spatial_rows].reshape(-1)
    temporal_share = share[0][spatial_rows:].reshape(-1)
    for term in share[1:]:
        spatial_share = spatial_share + term[:spatial_rows].reshape(-1)
        temporal_share = temporal_share + term[spatial_rows:].reshape(-1)
    return (decoded, spatial_share, temporal_share)


def solution(mesh):
    placed = (
        P("dp", None, "space", None, None),
        P("dp"),
        P(),
        P(),
        P(),
        P(),
        P("dp", None),
        P("dp", None, "space", None, None),
    )
    return jax.shard_map(
        on_device,
        mesh=mesh,
        in_specs=placed,
        out_specs=(P("dp", None, "space", None, None), P(("dp", "space")), P(("dp", "space"))),
        check_vma=False,
    )
```
